32 devices in a mesh: groups: 2 (over y), expert: 16 (over z, x, core).
Axes of the slice: x: 2, y: 2, z: 4, core: 2. Of those that a mesh axis runs over, the one named last changes fastest.
Arguments:
- tokens: bfloat16 [2048, 2048], P(('groups', 'expert')), parts along dimension 0, may hold values from -6 to 6
- expert_ids: int32 [2048, 8], P(('groups', 'expert')), parts along dimension 0, may hold values from 0 to 15, all different within a row; in each aligned block of 64 rows (0 to 63, 64 to 127, ...) at most 48 rows name the same one
- gate_scores: float32 [2048, 8], P(('groups', 'expert')), parts along dimension 0, may hold values from 0.05 to 1
- host_expert: int32 [16], replicated, may hold values from 0 to 15, each once
- w_in: bfloat16 [16, 2048, 1536], P('expert'), may hold values from -0.125 to 0.125
- w_down: bfloat16 [16, 768, 2048], P('expert'), may hold values from -0.625 to 0.625
Outputs:
- mixed: bfloat16 [2048, 2048], P(('groups', 'expert')), parts along dimension 0
The draws below stay inside these ranges and needn't reach their ends.
There are 2 independent parts, one for each index of `groups`. The reference program is written for one: setup_inputs(seed, part) draws one part's arguments, and reference() takes and returns one part's arrays. A program takes and returns all parts, laid end to end along the dimension named above; an argument that names none is the same for every part. Nothing has to cross between parts.
Inputs may be any that keep to these rules, and one draw needn't show every extreme that they name: `expert_ids`: each token names 8 different experts; the tokens of one device name no expert more than 48 times, a bound that some block reaches. `host_expert`: each expert stands in exactly one slot.
All inputs are finite; a program needn't handle non-finite values.
Results may differ from the reference program's by a relative error of at most 0.0057.
Values may be sent and summed in bfloat16 or wider, within the bound.
No kernel may reach another device: no remote copies, remote signals or barrier semaphores. Data moves between devices by JAX's collectives and lax.ppermute only.
A program may use at most 64 MiB of HBM per device.

```python
import math
import jax
import jax.numpy as jnp
import numpy as np
from jax import lax

D = 2048
FF = 768
TOPK = 8
BLOCK = 128
TOK_DEV = 64
EXPERTS = 16
TOKENS = 1024
CAP = 48


def steps_of(stream_key, extent, split, least, high):
    def one(dim, parts):
        draws = jax.random.uniform(jax.random.fold_in(jax.random.fold_in(stream_key, 6), dim), (parts,), jnp.float32, least / len(split), high / len(split))
        return jnp.repeat(jnp.exp(draws), extent[dim] // parts).reshape((-1,) + (1,) * (len(extent) - dim - 1))

    gain = one(*split[0])
    for cut in split[1:]:
        gain = gain * one(*cut)
    return gain


def deal_out(own_key, own, number, rows, amount, top, most, skew):
    sequence = jax.random.permutation(own_key, amount)
    crowded, ordinary = shares(amount, rows * top, most, skew, True), shares(amount, rows * top, most, skew, False)
    places = jnp.arange(amount)

    def named(sizes, turn):
        used = int((sizes > 0).sum())
        fixed = max(1, used // 4)
        moved = fixed + (places - fixed + turn * (used - fixed)) % max(1, amount - fixed)
        return jnp.zeros((amount,), jnp.int32).at[sequence[jnp.where(places < fixed, places, moved)]].set(jnp.asarray(sizes, jnp.int32))

    sizes = jnp.where(number % 4 == 0, named(crowded, number // 4), named(ordinary, number - number // 4 - 1))
    mixed = jax.random.permutation(jax.random.fold_in(own, 3), amount)
    source_of, sink = mixed[0:amount // 2 * 2:2], mixed[1:amount // 2 * 2:2]
    margin = jnp.minimum(sizes[source_of] - 1, most - sizes[sink]) // 2
    margin = jnp.where((source_of == sequence[0]) | (sink == sequence[0]) | (sizes[sink] == 0), 0, jnp.maximum(margin, 0))
    moved = jax.random.randint(jax.random.fold_in(own, 4), (amount // 2,), 0, 1 << 20) % (margin + 1)
    sizes = sizes.at[source_of].add(-moved).at[sink].add(moved)
    members = jnp.searchsorted(jnp.cumsum(sizes), jnp.arange(rows * top), side="right").astype(jnp.int32)
    listing = members.reshape(top, rows).T
    listing = listing[jax.random.permutation(jax.random.fold_in(own, 1), rows)]
    turn = jax.random.randint(jax.random.fold_in(own, 2), (rows, 1), 0, top)
    return jnp.take_along_axis(listing, (jnp.arange(top)[None, :] + turn) % top, axis=1)


def shares(count, total, limit, skew, full):
    loads = [(1 << 20) // math.isqrt(rank ** skew) + 1 for rank in range(1, count + 1)]
    largest = limit if full else min(limit, max(-(-total // count), total * loads[0] // sum(loads)))
    least = 1 if total - largest >= count - 1 else 0
    given, rest = [largest] + [least] * (count - 1), total - largest - least * (count - 1)
    while rest > 0:
        free = [i for i in range(1, count) if given[i] < largest] or [i for i in range(1, count) if given[i] < limit]
        whole, left = sum([loads[i] for i in free]), rest
        for i in free:
            addition = min(limit - given[i], max(1, left * loads[i] // whole), rest)
            given[i] = given[i] + addition
            rest = rest - addition
    return np.array(given)


def normal_values(own_key, shape, width, limit, pieces=(), kind=jnp.bfloat16):
    result = jax.random.normal(own_key, shape, jnp.float32) * width
    if len(pieces) > 0:
        result = steps_of(own_key, shape, pieces, -0.22, 0.18) * result
    return jnp.clip(result, min=-limit, max=limit).astype(kind)


def setup_inputs(seed: int = 0, part: int = 0) -> dict:
    arg_keys = jax.random.split(jax.random.key(seed), 7)
    own_keys = jax.random.split(jax.random.fold_in(arg_keys[6], part), 7)
    tokens = normal_values(own_keys[0], (TOKENS, D), 1.0, 6.0, ((0, 16),))
    expert_ids_keys = jax.random.split(jax.random.fold_in(own_keys[1], 1), TOKENS // TOK_DEV)
    expert_ids_turns = jax.random.permutation(jax.random.fold_in(own_keys[1], 3), TOKENS // TOK_DEV)
    expert_ids = jax.vmap(lambda own, number: deal_out(jax.random.fold_in(own_keys[1], 2), own, number, TOK_DEV, EXPERTS, TOPK, CAP, 2))(expert_ids_keys, expert_ids_turns).reshape((TOKENS, TOPK))
    gate_scores = jnp.clip(0.05 + 0.95 * jax.random.uniform(own_keys[2], (TOKENS, TOPK), jnp.float32) ** steps_of(own_keys[2], (TOKENS, TOPK), ((0, 16),), -0.2, 0.2), 0.05, 1.0)
    host_expert = jax.random.permutation(arg_keys[3], EXPERTS).astype(jnp.int32)
    w_in = normal_values(arg_keys[4], (EXPERTS, D, 2 * FF), D ** -0.5, 0.125, ((0, 16),))
    w_down = normal_values(arg_keys[5], (EXPERTS, FF, D), (FF // 8) ** -0.5, 0.625, ((0, 16),))
    return dict(tokens=tokens, expert_ids=expert_ids, gate_scores=gate_scores, host_expert=host_expert, w_in=w_in, w_down=w_down)


def reference(tokens, expert_ids, gate_scores, host_expert, w_in, w_down):
    routed = TOKENS * TOPK
    slot_of = jnp.zeros((EXPERTS,), jnp.int32).at[host_expert].set(jnp.arange(EXPERTS, dtype=jnp.int32))
    flat_ids = expert_ids.reshape(-1).astype(jnp.int32)
    counts = jax.ops.segment_sum(jnp.ones((routed,), jnp.int32), flat_ids, num_segments=EXPERTS)
    padded = (counts + BLOCK - 1) // BLOCK * BLOCK
    pad_start = jnp.cumsum(padded) - padded
    start = jnp.cumsum(counts) - counts
    order = jnp.argsort(flat_ids, stable=True).astype(jnp.int32)
    sorted_ids = flat_ids[order]
    target = (pad_start[sorted_ids] + jnp.arange(routed, dtype=jnp.int32) - start[sorted_ids]).astype(jnp.int32)
    block_total = routed // BLOCK + EXPERTS
    source = jnp.full((block_total * BLOCK,), routed, jnp.int32).at[target].set(order)
    place = jnp.zeros((routed,), jnp.int32).at[order].set(target)
    pad_end = pad_start + padded
    block_first = jnp.arange(block_total, dtype=jnp.int32) * BLOCK
    block_expert = jnp.minimum(jnp.sum((pad_end[None, :] <= block_first[:, None]).astype(jnp.int32), axis=1), EXPERTS - 1).astype(jnp.int32)
    padded_tokens = jnp.concatenate([tokens, jnp.zeros((1, D), tokens.dtype)], axis=0)
    token_of = jnp.where(source < routed, source // TOPK, TOKENS).astype(jnp.int32)

    def one_block(operands):
        row_index, expert = operands
        rows_in = padded_tokens[row_index]
        holder = slot_of[expert]
        pair = jnp.dot(rows_in, w_in[holder], preferred_element_type=jnp.float32)
        active = (jax.nn.silu(pair[:, :FF]) * pair[:, FF:]).astype(jnp.bfloat16)
        return jnp.dot(active, w_down[holder], preferred_element_type=jnp.float32).astype(jnp.bfloat16)

    outputs = lax.map(one_block, (token_of.reshape(block_total, BLOCK), block_expert))
    expert_out = outputs.reshape(block_total * BLOCK, D)[place].reshape(TOKENS, TOPK, D)
    weights = gate_scores / jnp.sum(gate_scores, axis=1, keepdims=True)
    mixed = jnp.sum(weights[:, :, None] * expert_out.astype(jnp.float32), axis=1)
    return mixed.astype(jnp.bfloat16)
```

```python
import jax
import jax.numpy as jnp
import numpy as np
from jax import lax
from jax.sharding import Mesh, PartitionSpec as P


def expert_block(rows_in, gate_up, down_proj, hidden_width):
    pair = jnp.dot(rows_in, gate_up, preferred_element_type=jnp.float32)
    active = (jax.nn.silu(pair[:, :hidden_width]) * pair[:, hidden_width:]).astype(jnp.bfloat16)
    return jnp.dot(active, down_proj, preferred_element_type=jnp.float32).astype(jnp.bfloat16)


def shards(tokens, expert_ids, gate_scores, host_expert, w_in, w_down):
    tok_rows, width_model = tokens.shape
    top_count = expert_ids.shape[1]
    hosts = lax.axis_size("expert")
    experts = host_expert.shape[0]
    capacity = 3 * tok_rows * top_count // (2 * experts)
    hidden_width = w_down.shape[1]
    routed = tok_rows * top_count
    slots = hosts * capacity
    gate_up = w_in[0]
    down_proj = w_down[0]
    expert_range = jnp.arange(experts, dtype=jnp.int32)
    host_range = jnp.arange(hosts, dtype=jnp.int32)
    placed = (host_expert[:, None] == expert_range[None, :]).astype(jnp.int32)
    host_of = jnp.sum(placed * host_range[:, None], axis=0)
    flat_ids = expert_ids.reshape(-1)
    id_match = flat_ids[:, None] == expert_range[None, :]
    dest_host = jnp.sum(jnp.where(id_match, host_of[None, :], 0), axis=1)
    row_token = jnp.arange(routed, dtype=jnp.int32) // top_count
    padded_tokens = jnp.concatenate([tokens, jnp.zeros((1, width_model), tokens.dtype)], axis=0)
    earlier = (
        lax.broadcasted_iota(jnp.int32, (routed, routed), 0)
        > lax.broadcasted_iota(jnp.int32, (routed, routed), 1)
    ).astype(jnp.bfloat16)
    dest_match = dest_host[:, None] == host_range[None, :]
    before = jnp.dot(earlier, dest_match.astype(jnp.bfloat16), preferred_element_type=jnp.float32)
    position = jnp.sum(jnp.where(dest_match, before, 0.0), axis=1).astype(jnp.int32)
    slot_of_row = dest_host * capacity + position
    source_row = jnp.full((slots + 1,), tok_rows, jnp.int32).at[slot_of_row].set(row_token)[:slots]
    outgoing = padded_tokens[source_row].reshape(hosts, capacity, width_model)
    received = lax.all_to_all(outgoing, "expert", split_axis=0, concat_axis=0, tiled=True)
    flat_in = received.reshape(-1, width_model)
    served = expert_block(flat_in, gate_up, down_proj, hidden_width).reshape(received.shape)
    returned = lax.all_to_all(served, "expert", split_axis=0, concat_axis=0, tiled=True)
    expert_rows = returned.reshape(slots, width_model)[slot_of_row]
    weights = gate_scores / jnp.sum(gate_scores, axis=1, keepdims=True)
    mixed = jnp.sum(
        weights[:, :, None]
        * expert_rows.reshape(tok_rows, top_count, width_model).astype(jnp.float32),
        axis=1,
    )
    return mixed.astype(jnp.bfloat16)


AXES = ("ez", "ex", "ec")


def dense_shards(tokens, expert_ids, gate_scores, host_expert, w_in, w_down):
    tok_rows, width_model = tokens.shape
    hidden_width = w_down.shape[1]
    experts = host_expert.shape[0]
    me = (lax.axis_index("ez") * lax.axis_size("ex") + lax.axis_index("ex")) * lax.axis_size("ec") + lax.axis_index("ec")
    my_expert = jnp.sum(jnp.where(jnp.arange(experts, dtype=jnp.int32) == me, host_expert, 0))
    weights = gate_scores / jnp.sum(gate_scores, axis=1, keepdims=True)
    rows = tokens
    gate = expert_ids
    score = weights
    for axis in AXES:
        rows = lax.all_gather(rows, axis, tiled=True)
        gate = lax.all_gather(gate, axis, tiled=True)
        score = lax.all_gather(score, axis, tiled=True)
    mine_all = jnp.sum(jnp.where(gate == my_expert, score, 0.0), axis=1)
    out = expert_block(rows, w_in[0], w_down[0], hidden_width)
    part = (out.astype(jnp.float32) * mine_all[:, None]).astype(jnp.bfloat16)
    for axis in AXES[::-1]:
        part = lax.psum_scatter(part, axis, scatter_dimension=0, tiled=True)
    return part


def factor_expert(mesh):
    row = mesh.devices[0]
    try:
        cores = len({d.core_on_chip for d in row})
        xs = len({d.coords[0] for d in row})
        zs = len({d.coords[2] for d in row})
    except AttributeError:
        return None
    if cores * xs * zs != row.shape[0]:
        return None
    return zs, xs, cores


def solution(mesh):
    placed = (
        P(("groups", "expert"), None),
        P(("groups", "expert"), None),
        P(("groups", "expert"), None),
        P(),
        P("expert", None, None),
        P("expert", None, None),
    )
    factors = factor_expert(mesh)
    if factors is None or mesh.shape["expert"] > 16:
        return jax.shard_map(
            shards, mesh=mesh, in_specs=placed, out_specs=P(("groups", "expert"), None), check_vma=False
        )
    sub = Mesh(mesh.devices.reshape((mesh.shape["groups"],) + factors), ("groups",) + AXES)
    rows = P(("groups",) + AXES, None)
    placed = (rows, rows, rows, P(), P(AXES, None, None), P(AXES, None, None))
    return jax.shard_map(dense_shards, mesh=sub, in_specs=placed, out_specs=rows, check_vma=False)
```

```python
import jax
import jax.numpy as jnp
import numpy as np
from jax import lax
from jax.sharding import Mesh, PartitionSpec as P


def expert_block(rows_in, gate_up, down_proj, hidden_width):
    pair = jnp.dot(rows_in, gate_up, preferred_element_type=jnp.float32)
    active = (jax.nn.silu(pair[:, :hidden_width]) * pair[:, hidden_width:]).astype(jnp.bfloat16)
    return jnp.dot(active, down_proj, preferred_element_type=jnp.float32).astype(jnp.bfloat16)


def shards(tokens, expert_ids, gate_scores, host_expert, w_in, w_down):
    tok_rows, width_model = tokens.shape
    top_count = expert_ids.shape[1]
    hosts = lax.axis_size("expert")
    experts = host_expert.shape[0]
    capacity = 3 * tok_rows * top_count // (2 * experts)
    hidden_width = w_down.shape[1]
    routed = tok_rows * top_count
    slots = hosts * capacity
    gate_up = w_in[0]
    down_proj = w_down[0]
    expert_range = jnp.arange(experts, dtype=jnp.int32)
    host_range = jnp.arange(hosts, dtype=jnp.int32)
    placed = (host_expert[:, None] == expert_range[None, :]).astype(jnp.int32)
    host_of = jnp.sum(placed * host_range[:, None], axis=0)
    flat_ids = expert_ids.reshape(-1)
    id_match = flat_ids[:, None] == expert_range[None, :]
    dest_host = jnp.sum(jnp.where(id_match, host_of[None, :], 0), axis=1)
    row_token = jnp.arange(routed, dtype=jnp.int32) // top_count
    padded_tokens = jnp.concatenate([tokens, jnp.zeros((1, width_model), tokens.dtype)], axis=0)
    earlier = (
        lax.broadcasted_iota(jnp.int32, (routed, routed), 0)
        > lax.broadcasted_iota(jnp.int32, (routed, routed), 1)
    ).astype(jnp.bfloat16)
    dest_match = dest_host[:, None] == host_range[None, :]
    before = jnp.dot(earlier, dest_match.astype(jnp.bfloat16), preferred_element_type=jnp.float32)
    position = jnp.sum(jnp.where(dest_match, before, 0.0), axis=1).astype(jnp.int32)
    slot_of_row = dest_host * capacity + position
    source_row = jnp.full((slots + 1,), tok_rows, jnp.int32).at[slot_of_row].set(row_token)[:slots]
    outgoing = padded_tokens[source_row].reshape(hosts, capacity, width_model)
    received = lax.all_to_all(outgoing, "expert", split_axis=0, concat_axis=0, tiled=True)
    flat_in = received.reshape(-1, width_model)
    served = expert_block(flat_in, gate_up, down_proj, hidden_width).reshape(received.shape)
    returned = lax.all_to_all(served, "expert", split_axis=0, concat_axis=0, tiled=True)
    expert_rows = returned.reshape(slots, width_model)[slot_of_row]
    weights = gate_scores / jnp.sum(gate_scores, axis=1, keepdims=True)
    mixed = jnp.sum(
        weights[:, :, None]
        * expert_rows.reshape(tok_rows, top_count, width_model).astype(jnp.float32),
        axis=1,
    )
    return mixed.astype(jnp.bfloat16)


AXES = ("ez", "ex", "ec")


def gather_stage(blocks, axis, size):
    got = [blocks]
    for shift in range(1, size):
        pairs = [(i, (i + shift) % size) for i in range(size)]
        got.append(jax.tree.map(lambda b: lax.ppermute(b, axis, pairs), blocks))
    return jax.tree.map(lambda *parts: jnp.concatenate(parts, axis=0), *got)


def scatter_stage(part, axis, size):
    pieces = jnp.split(part, size, axis=0)
    total = pieces[0].astype(jnp.float32)
    for shift in range(1, size):
        pairs = [(i, (i - shift) % size) for i in range(size)]
        total = total + lax.ppermute(pieces[shift].astype(jnp.bfloat16), axis, pairs).astype(jnp.float32)
    return total


def dense_shards(tokens, expert_ids, gate_scores, host_expert, w_in, w_down):
    hidden_width = w_down.shape[1]
    experts = host_expert.shape[0]
    sizes = [lax.axis_size(a) for a in AXES]
    me = (lax.axis_index("ez") * sizes[1] + lax.axis_index("ex")) * sizes[2] + lax.axis_index("ec")
    my_expert = jnp.sum(jnp.where(jnp.arange(experts, dtype=jnp.int32) == me, host_expert, 0))
    weights = gate_scores / jnp.sum(gate_scores, axis=1, keepdims=True)
    blocks = (tokens, expert_ids, weights)
    for axis, size in zip(AXES, sizes):
        blocks = gather_stage(blocks, axis, size)
    rows, gate, score = blocks
    mine = jnp.sum(jnp.where(gate == my_expert, score, 0.0), axis=1)
    out = expert_block(rows, w_in[0], w_down[0], hidden_width)
    part = out.astype(jnp.float32) * mine[:, None]
    for axis, size in list(zip(AXES, sizes))[::-1]:
        part = scatter_stage(part, axis, size)
    return part.astype(jnp.bfloat16)


def factor_expert(mesh):
    row = mesh.devices[0]
    try:
        cores = len({d.core_on_chip for d in row})
        xs = len({d.coords[0] for d in row})
        zs = len({d.coords[2] for d in row})
    except AttributeError:
        return None
    if cores * xs * zs != row.shape[0]:
        return None
    return zs, xs, cores


def solution(mesh):
    placed = (
        P(("groups", "expert"), None),
        P(("groups", "expert"), None),
        P(("groups", "expert"), None),
        P(),
        P("expert", None, None),
        P("expert", None, None),
    )
    factors = factor_expert(mesh)
    if factors is None or mesh.shape["expert"] > 16:
        return jax.shard_map(
            shards, mesh=mesh, in_specs=placed, out_specs=P(("groups", "expert"), None), check_vma=False
        )
    sub = Mesh(mesh.devices.reshape((mesh.shape["groups"],) + factors), ("groups",) + AXES)
    rows = P(("groups",) + AXES, None)
    placed = (rows, rows, rows, P(), P(AXES, None, None), P(AXES, None, None))
    return jax.shard_map(dense_shards, mesh=sub, in_specs=placed, out_specs=rows, check_vma=False)
```

```python
import jax
import jax.numpy as jnp
import numpy as np
from jax import lax
from jax.sharding import Mesh, PartitionSpec as P


def expert_block(rows_in, gate_up, down_proj, hidden_width):
    pair = jnp.dot(rows_in, gate_up, preferred_element_type=jnp.float32)
    active = (jax.nn.silu(pair[:, :hidden_width]) * pair[:, hidden_width:]).astype(jnp.bfloat16)
    return jnp.dot(active, down_proj, preferred_element_type=jnp.float32).astype(jnp.bfloat16)


def shards(tokens, expert_ids, gate_scores, host_expert, w_in, w_down):
    tok_rows, width_model = tokens.shape
    top_count = expert_ids.shape[1]
    hosts = lax.axis_size("expert")
    experts = host_expert.shape[0]
    capacity = 3 * tok_rows * top_count // (2 * experts)
    hidden_width = w_down.shape[1]
    routed = tok_rows * top_count
    slots = hosts * capacity
    gate_up = w_in[0]
    down_proj = w_down[0]
    expert_range = jnp.arange(experts, dtype=jnp.int32)
    host_range = jnp.arange(hosts, dtype=jnp.int32)
    placed = (host_expert[:, None] == expert_range[None, :]).astype(jnp.int32)
    host_of = jnp.sum(placed * host_range[:, None], axis=0)
    flat_ids = expert_ids.reshape(-1)
    id_match = flat_ids[:, None] == expert_range[None, :]
    dest_host = jnp.sum(jnp.where(id_match, host_of[None, :], 0), axis=1)
    row_token = jnp.arange(routed, dtype=jnp.int32) // top_count
    padded_tokens = jnp.concatenate([tokens, jnp.zeros((1, width_model), tokens.dtype)], axis=0)
    earlier = (
        lax.broadcasted_iota(jnp.int32, (routed, routed), 0)
        > lax.broadcasted_iota(jnp.int32, (routed, routed), 1)
    ).astype(jnp.bfloat16)
    dest_match = dest_host[:, None] == host_range[None, :]
    before = jnp.dot(earlier, dest_match.astype(jnp.bfloat16), preferred_element_type=jnp.float32)
    position = jnp.sum(jnp.where(dest_match, before, 0.0), axis=1).astype(jnp.int32)
    slot_of_row = dest_host * capacity + position
    source_row = jnp.full((slots + 1,), tok_rows, jnp.int32).at[slot_of_row].set(row_token)[:slots]
    outgoing = padded_tokens[source_row].reshape(hosts, capacity, width_model)
    received = lax.all_to_all(outgoing, "expert", split_axis=0, concat_axis=0, tiled=True)
    flat_in = received.reshape(-1, width_model)
    served = expert_block(flat_in, gate_up, down_proj, hidden_width).reshape(received.shape)
    returned = lax.all_to_all(served, "expert", split_axis=0, concat_axis=0, tiled=True)
    expert_rows = returned.reshape(slots, width_model)[slot_of_row]
    weights = gate_scores / jnp.sum(gate_scores, axis=1, keepdims=True)
    mixed = jnp.sum(
        weights[:, :, None]
        * expert_rows.reshape(tok_rows, top_count, width_model).astype(jnp.float32),
        axis=1,
    )
    return mixed.astype(jnp.bfloat16)


AXES = ("ez", "ex", "ec")


def gather_stage(blocks, axis, size):
    got = [blocks]
    for shift in range(1, size):
        pairs = [(i, (i + shift) % size) for i in range(size)]
        got.append(jax.tree.map(lambda b: lax.ppermute(b, axis, pairs), blocks))
    return jax.tree.map(lambda *parts: jnp.concatenate(parts, axis=0), *got)


def scatter_stage(part, axis, size):
    pieces = jnp.split(part, size, axis=0)
    total = pieces[0].astype(jnp.float32)
    for shift in range(1, size):
        pairs = [(i, (i - shift) % size) for i in range(size)]
        total = total + lax.ppermute(pieces[shift].astype(jnp.bfloat16), axis, pairs).astype(jnp.float32)
    return total


def dense_shards(tokens, expert_ids, gate_scores, host_expert, w_in, w_down):
    hidden_width = w_down.shape[1]
    experts = host_expert.shape[0]
    sizes = [lax.axis_size(a) for a in AXES]
    me = (lax.axis_index("ez") * sizes[1] + lax.axis_index("ex")) * sizes[2] + lax.axis_index("ec")
    my_expert = jnp.sum(jnp.where(jnp.arange(experts, dtype=jnp.int32) == me, host_expert, 0))
    weights = gate_scores / jnp.sum(gate_scores, axis=1, keepdims=True)
    streams = [
        jax.tree.map(lambda a: jnp.split(a, STREAMS, axis=0)[k], (tokens, expert_ids, weights))
        for k in range(STREAMS)
    ]
    results = []
    held = None
    for blocks in streams:
        if held is not None:
            held, blocks = lax.optimization_barrier((held, blocks))
        blocks = gather_stage(blocks, AXES[0], sizes[0])
        held = blocks[0]
        for axis, size in zip(AXES[1:], sizes[1:]):
            blocks = gather_stage(blocks, axis, size)
        rows, gate, score = blocks
        mine = jnp.sum(jnp.where(gate == my_expert, score, 0.0), axis=1)
        out = expert_block(rows, w_in[0], w_down[0], hidden_width)
        part = out.astype(jnp.float32) * mine[:, None]
        for axis, size in list(zip(AXES, sizes))[::-1]:
            part = scatter_stage(part, axis, size)
        results.append(part)
    return jnp.concatenate(results, axis=0).astype(jnp.bfloat16)


STREAMS = 2


def factor_expert(mesh):
    row = mesh.devices[0]
    try:
        cores = len({d.core_on_chip for d in row})
        xs = len({d.coords[0] for d in row})
        zs = len({d.coords[2] for d in row})
    except AttributeError:
        return None
    if cores * xs * zs != row.shape[0]:
        return None
    return zs, xs, cores


def solution(mesh):
    placed = (
        P(("groups", "expert"), None),
        P(("groups", "expert"), None),
        P(("groups", "expert"), None),
        P(),
        P("expert", None, None),
        P("expert", None, None),
    )
    factors = factor_expert(mesh)
    if factors is None or mesh.shape["expert"] > 16:
        return jax.shard_map(
            shards, mesh=mesh, in_specs=placed, out_specs=P(("groups", "expert"), None), check_vma=False
        )
    sub = Mesh(mesh.devices.reshape((mesh.shape["groups"],) + factors), ("groups",) + AXES)
    rows = P(("groups",) + AXES, None)
    placed = (rows, rows, rows, P(), P(AXES, None, None), P(AXES, None, None))
    return jax.shard_map(dense_shards, mesh=sub, in_specs=placed, out_specs=rows, check_vma=False)
```

```python
import jax
import jax.numpy as jnp
import numpy as np
from jax import lax
from jax.sharding import Mesh, PartitionSpec as P


def expert_block(rows_in, gate_up, down_proj, hidden_width):
    pair = jnp.dot(rows_in, gate_up, preferred_element_type=jnp.float32)
    active = (jax.nn.silu(pair[:, :hidden_width]) * pair[:, hidden_width:]).astype(jnp.bfloat16)
    return jnp.dot(active, down_proj, preferred_element_type=jnp.float32).astype(jnp.bfloat16)


def shards(tokens, expert_ids, gate_scores, host_expert, w_in, w_down):
    tok_rows, width_model = tokens.shape
    top_count = expert_ids.shape[1]
    hosts = lax.axis_size("expert")
    experts = host_expert.shape[0]
    capacity = 3 * tok_rows * top_count // (2 * experts)
    hidden_width = w_down.shape[1]
    routed = tok_rows * top_count
    slots = hosts * capacity
    gate_up = w_in[0]
    down_proj = w_down[0]
    expert_range = jnp.arange(experts, dtype=jnp.int32)
    host_range = jnp.arange(hosts, dtype=jnp.int32)
    placed = (host_expert[:, None] == expert_range[None, :]).astype(jnp.int32)
    host_of = jnp.sum(placed * host_range[:, None], axis=0)
    flat_ids = expert_ids.reshape(-1)
    id_match = flat_ids[:, None] == expert_range[None, :]
    dest_host = jnp.sum(jnp.where(id_match, host_of[None, :], 0), axis=1)
    row_token = jnp.arange(routed, dtype=jnp.int32) // top_count
    padded_tokens = jnp.concatenate([tokens, jnp.zeros((1, width_model), tokens.dtype)], axis=0)
    earlier = (
        lax.broadcasted_iota(jnp.int32, (routed, routed), 0)
        > lax.broadcasted_iota(jnp.int32, (routed, routed), 1)
    ).astype(jnp.bfloat16)
    dest_match = dest_host[:, None] == host_range[None, :]
    before = jnp.dot(earlier, dest_match.astype(jnp.bfloat16), preferred_element_type=jnp.float32)
    position = jnp.sum(jnp.where(dest_match, before, 0.0), axis=1).astype(jnp.int32)
    slot_of_row = dest_host * capacity + position
    source_row = jnp.full((slots + 1,), tok_rows, jnp.int32).at[slot_of_row].set(row_token)[:slots]
    outgoing = padded_tokens[source_row].reshape(hosts, capacity, width_model)
    received = lax.all_to_all(outgoing, "expert", split_axis=0, concat_axis=0, tiled=True)
    flat_in = received.reshape(-1, width_model)
    served = expert_block(flat_in, gate_up, down_proj, hidden_width).reshape(received.shape)
    returned = lax.all_to_all(served, "expert", split_axis=0, concat_axis=0, tiled=True)
    expert_rows = returned.reshape(slots, width_model)[slot_of_row]
    weights = gate_scores / jnp.sum(gate_scores, axis=1, keepdims=True)
    mixed = jnp.sum(
        weights[:, :, None]
        * expert_rows.reshape(tok_rows, top_count, width_model).astype(jnp.float32),
        axis=1,
    )
    return mixed.astype(jnp.bfloat16)


AXES = ("ez", "ex", "ec")


def gather_stage(block, axis, size):
    got = [block]
    for shift in range(1, size):
        pairs = [(i, (i + shift) % size) for i in range(size)]
        got.append(lax.ppermute(block, axis, pairs))
    return jnp.concatenate(got, axis=0)


def scatter_stage(part, axis, size):
    pieces = jnp.split(part, size, axis=0)
    total = pieces[0].astype(jnp.float32)
    for shift in range(1, size):
        pairs = [(i, (i - shift) % size) for i in range(size)]
        total = total + lax.ppermute(pieces[shift].astype(jnp.bfloat16), axis, pairs).astype(jnp.float32)
    return total


def dense_shards(tokens, expert_ids, gate_scores, host_expert, w_in, w_down):
    tok_rows, width_model = tokens.shape
    hidden_width = w_down.shape[1]
    experts = host_expert.shape[0]
    sizes = [lax.axis_size(a) for a in AXES]
    hosts = sizes[0] * sizes[1] * sizes[2]
    me = (lax.axis_index("ez") * sizes[1] + lax.axis_index("ex")) * sizes[2] + lax.axis_index("ec")
    weights = gate_scores / jnp.sum(gate_scores, axis=1, keepdims=True)
    chosen = expert_ids[:, :, None] == host_expert[None, None, :]
    per_host = jnp.sum(jnp.where(chosen, weights[:, :, None], 0.0), axis=1)
    hi = per_host.astype(jnp.bfloat16)
    rest = per_host - hi.astype(jnp.float32)
    lo = rest.astype(jnp.bfloat16)
    lo2 = (rest - lo.astype(jnp.float32)).astype(jnp.bfloat16)
    extra = -(-3 * hosts // 128) * 128
    meta = jnp.concatenate([hi, lo, lo2, jnp.zeros((tok_rows, extra - 3 * hosts), jnp.bfloat16)], axis=1)
    carried = jnp.concatenate([tokens, meta], axis=1)
    pick = (jnp.arange(hosts, dtype=jnp.int32) == me).astype(jnp.float32)
    results = []
    held = None
    for rows in jnp.split(carried, STREAMS, axis=0):
        if held is not None:
            held, rows = lax.optimization_barrier((held, rows))
        rows = gather_stage(rows, AXES[0], sizes[0])
        held = rows
        for axis, size in zip(AXES[1:], sizes[1:]):
            rows = gather_stage(rows, axis, size)
        tail = rows[:, width_model:width_model + 3 * hosts].astype(jnp.float32)
        gate = tail[:, :hosts] + tail[:, hosts:2 * hosts] + tail[:, 2 * hosts:]
        mine = jnp.sum(gate * pick[None, :], axis=1)
        out = expert_block(rows[:, :width_model], w_in[0], w_down[0], hidden_width)
        part = out.astype(jnp.float32) * mine[:, None]
        for axis, size in list(zip(AXES, sizes))[::-1]:
            part = scatter_stage(part, axis, size)
        results.append(part)
    return jnp.concatenate(results, axis=0).astype(jnp.bfloat16)


STREAMS = 2


def factor_expert(mesh):
    row = mesh.devices[0]
    try:
        cores = len({d.core_on_chip for d in row})
        xs = len({d.coords[0] for d in row})
        zs = len({d.coords[2] for d in row})
    except AttributeError:
        return None
    if cores * xs * zs != row.shape[0]:
        return None
    return zs, xs, cores


def solution(mesh):
    placed = (
        P(("groups", "expert"), None),
        P(("groups", "expert"), None),
        P(("groups", "expert"), None),
        P(),
        P("expert", None, None),
        P("expert", None, None),
    )
    factors = factor_expert(mesh)
    if factors is None or mesh.shape["expert"] > 16:
        return jax.shard_map(
            shards, mesh=mesh, in_specs=placed, out_specs=P(("groups", "expert"), None), check_vma=False
        )
    sub = Mesh(mesh.devices.reshape((mesh.shape["groups"],) + factors), ("groups",) + AXES)
    rows = P(("groups",) + AXES, None)
    placed = (rows, rows, rows, P(), P(AXES, None, None), P(AXES, None, None))
    return jax.shard_map(dense_shards, mesh=sub, in_specs=placed, out_specs=rows, check_vma=False)
```

```python
import jax
import jax.numpy as jnp
import numpy as np
from jax import lax
from jax.sharding import Mesh, PartitionSpec as P


def expert_block(rows_in, gate_up, down_proj, hidden_width):
    pair = jnp.dot(rows_in, gate_up, preferred_element_type=jnp.float32)
    active = (jax.nn.silu(pair[:, :hidden_width]) * pair[:, hidden_width:]).astype(jnp.bfloat16)
    return jnp.dot(active, down_proj, preferred_element_type=jnp.float32).astype(jnp.bfloat16)


def shards(tokens, expert_ids, gate_scores, host_expert, w_in, w_down):
    tok_rows, width_model = tokens.shape
    top_count = expert_ids.shape[1]
    hosts = lax.axis_size("expert")
    experts = host_expert.shape[0]
    capacity = 3 * tok_rows * top_count // (2 * experts)
    hidden_width = w_down.shape[1]
    routed = tok_rows * top_count
    slots = hosts * capacity
    gate_up = w_in[0]
    down_proj = w_down[0]
    expert_range = jnp.arange(experts, dtype=jnp.int32)
    host_range = jnp.arange(hosts, dtype=jnp.int32)
    placed = (host_expert[:, None] == expert_range[None, :]).astype(jnp.int32)
    host_of = jnp.sum(placed * host_range[:, None], axis=0)
    flat_ids = expert_ids.reshape(-1)
    id_match = flat_ids[:, None] == expert_range[None, :]
    dest_host = jnp.sum(jnp.where(id_match, host_of[None, :], 0), axis=1)
    row_token = jnp.arange(routed, dtype=jnp.int32) // top_count
    padded_tokens = jnp.concatenate([tokens, jnp.zeros((1, width_model), tokens.dtype)], axis=0)
    earlier = (
        lax.broadcasted_iota(jnp.int32, (routed, routed), 0)
        > lax.broadcasted_iota(jnp.int32, (routed, routed), 1)
    ).astype(jnp.bfloat16)
    dest_match = dest_host[:, None] == host_range[None, :]
    before = jnp.dot(earlier, dest_match.astype(jnp.bfloat16), preferred_element_type=jnp.float32)
    position = jnp.sum(jnp.where(dest_match, before, 0.0), axis=1).astype(jnp.int32)
    slot_of_row = dest_host * capacity + position
    source_row = jnp.full((slots + 1,), tok_rows, jnp.int32).at[slot_of_row].set(row_token)[:slots]
    outgoing = padded_tokens[source_row].reshape(hosts, capacity, width_model)
    received = lax.all_to_all(outgoing, "expert", split_axis=0, concat_axis=0, tiled=True)
    flat_in = received.reshape(-1, width_model)
    served = expert_block(flat_in, gate_up, down_proj, hidden_width).reshape(received.shape)
    returned = lax.all_to_all(served, "expert", split_axis=0, concat_axis=0, tiled=True)
    expert_rows = returned.reshape(slots, width_model)[slot_of_row]
    weights = gate_scores / jnp.sum(gate_scores, axis=1, keepdims=True)
    mixed = jnp.sum(
        weights[:, :, None]
        * expert_rows.reshape(tok_rows, top_count, width_model).astype(jnp.float32),
        axis=1,
    )
    return mixed.astype(jnp.bfloat16)


AXES = ("ez", "ex", "ec")


def gather_stage(block, axis, size):
    got = [block]
    for shift in range(1, size):
        pairs = [(i, (i + shift) % size) for i in range(size)]
        got.append(lax.ppermute(block, axis, pairs))
    return jnp.concatenate(got, axis=0)


def scatter_stage(part, axis, size):
    pieces = jnp.split(part, size, axis=0)
    total = pieces[0].astype(jnp.float32)
    for shift in range(1, size):
        pairs = [(i, (i - shift) % size) for i in range(size)]
        total = total + lax.ppermute(pieces[shift].astype(jnp.bfloat16), axis, pairs).astype(jnp.float32)
    return total


def dense_shards(tokens, expert_ids, gate_scores, host_expert, w_in, w_down):
    tok_rows, width_model = tokens.shape
    hidden_width = w_down.shape[1]
    experts = host_expert.shape[0]
    sizes = [lax.axis_size(a) for a in AXES]
    hosts = sizes[0] * sizes[1] * sizes[2]
    me = (lax.axis_index("ez") * sizes[1] + lax.axis_index("ex")) * sizes[2] + lax.axis_index("ec")
    weights = gate_scores / jnp.sum(gate_scores, axis=1, keepdims=True)
    chosen = expert_ids[:, :, None] == host_expert[None, None, :]
    per_host = jnp.sum(jnp.where(chosen, weights[:, :, None], 0.0), axis=1)
    hi = lax.reduce_precision(per_host, exponent_bits=8, mantissa_bits=7)
    rest = per_host - hi
    lo = lax.reduce_precision(rest, exponent_bits=8, mantissa_bits=7)
    lo2 = rest - lo
    extra = -(-3 * hosts // 128) * 128
    meta = jnp.concatenate([hi, lo, lo2, jnp.zeros((tok_rows, extra - 3 * hosts), jnp.float32)], axis=1)
    meta = meta.astype(jnp.bfloat16)
    carried = jnp.concatenate([tokens, meta], axis=1)
    pick = (jnp.arange(hosts, dtype=jnp.int32) == me).astype(jnp.float32)
    results = []
    held = None
    for rows in jnp.split(carried, STREAMS, axis=0):
        if held is not None:
            held, rows = lax.optimization_barrier((held, rows))
        rows = gather_stage(rows, AXES[0], sizes[0])
        held = rows
        for axis, size in zip(AXES[1:], sizes[1:]):
            rows = gather_stage(rows, axis, size)
        tail = rows[:, width_model:width_model + 3 * hosts].astype(jnp.float32)
        gate = tail[:, :hosts] + tail[:, hosts:2 * hosts] + tail[:, 2 * hosts:]
        mine = jnp.sum(gate * pick[None, :], axis=1)
        out = expert_block(rows[:, :width_model], w_in[0], w_down[0], hidden_width)
        part = out.astype(jnp.float32) * mine[:, None]
        for axis, size in list(zip(AXES, sizes))[::-1]:
            part = scatter_stage(part, axis, size)
        results.append(part)
    return jnp.concatenate(results, axis=0).astype(jnp.bfloat16)


STREAMS = 2


def factor_expert(mesh):
    row = mesh.devices[0]
    try:
        cores = len({d.core_on_chip for d in row})
        xs = len({d.coords[0] for d in row})
        zs = len({d.coords[2] for d in row})
    except AttributeError:
        return None
    if cores * xs * zs != row.shape[0]:
        return None
    return zs, xs, cores


def solution(mesh):
    placed = (
        P(("groups", "expert"), None),
        P(("groups", "expert"), None),
        P(("groups", "expert"), None),
        P(),
        P("expert", None, None),
        P("expert", None, None),
    )
    factors = factor_expert(mesh)
    if factors is None or mesh.shape["expert"] > 16:
        return jax.shard_map(
            shards, mesh=mesh, in_specs=placed, out_specs=P(("groups", "expert"), None), check_vma=False
        )
    sub = Mesh(mesh.devices.reshape((mesh.shape["groups"],) + factors), ("groups",) + AXES)
    rows = P(("groups",) + AXES, None)
    placed = (rows, rows, rows, P(), P(AXES, None, None), P(AXES, None, None))
    return jax.shard_map(dense_shards, mesh=sub, in_specs=placed, out_specs=rows, check_vma=False)
```

```python
import jax
import jax.numpy as jnp
import numpy as np
from jax import lax
from jax.sharding import Mesh, PartitionSpec as P


def expert_block(rows_in, gate_up, down_proj, hidden_width):
    pair = jnp.dot(rows_in, gate_up, preferred_element_type=jnp.float32)
    active = (jax.nn.silu(pair[:, :hidden_width]) * pair[:, hidden_width:]).astype(jnp.bfloat16)
    return jnp.dot(active, down_proj, preferred_element_type=jnp.float32).astype(jnp.bfloat16)


def shards(tokens, expert_ids, gate_scores, host_expert, w_in, w_down):
    tok_rows, width_model = tokens.shape
    top_count = expert_ids.shape[1]
    hosts = lax.axis_size("expert")
    experts = host_expert.shape[0]
    capacity = 3 * tok_rows * top_count // (2 * experts)
    hidden_width = w_down.shape[1]
    routed = tok_rows * top_count
    slots = hosts * capacity
    gate_up = w_in[0]
    down_proj = w_down[0]
    expert_range = jnp.arange(experts, dtype=jnp.int32)
    host_range = jnp.arange(hosts, dtype=jnp.int32)
    placed = (host_expert[:, None] == expert_range[None, :]).astype(jnp.int32)
    host_of = jnp.sum(placed * host_range[:, None], axis=0)
    flat_ids = expert_ids.reshape(-1)
    id_match = flat_ids[:, None] == expert_range[None, :]
    dest_host = jnp.sum(jnp.where(id_match, host_of[None, :], 0), axis=1)
    row_token = jnp.arange(routed, dtype=jnp.int32) // top_count
    padded_tokens = jnp.concatenate([tokens, jnp.zeros((1, width_model), tokens.dtype)], axis=0)
    earlier = (
        lax.broadcasted_iota(jnp.int32, (routed, routed), 0)
        > lax.broadcasted_iota(jnp.int32, (routed, routed), 1)
    ).astype(jnp.bfloat16)
    dest_match = dest_host[:, None] == host_range[None, :]
    before = jnp.dot(earlier, dest_match.astype(jnp.bfloat16), preferred_element_type=jnp.float32)
    position = jnp.sum(jnp.where(dest_match, before, 0.0), axis=1).astype(jnp.int32)
    slot_of_row = dest_host * capacity + position
    source_row = jnp.full((slots + 1,), tok_rows, jnp.int32).at[slot_of_row].set(row_token)[:slots]
    outgoing = padded_tokens[source_row].reshape(hosts, capacity, width_model)
    received = lax.all_to_all(outgoing, "expert", split_axis=0, concat_axis=0, tiled=True)
    flat_in = received.reshape(-1, width_model)
    served = expert_block(flat_in, gate_up, down_proj, hidden_width).reshape(received.shape)
    returned = lax.all_to_all(served, "expert", split_axis=0, concat_axis=0, tiled=True)
    expert_rows = returned.reshape(slots, width_model)[slot_of_row]
    weights = gate_scores / jnp.sum(gate_scores, axis=1, keepdims=True)
    mixed = jnp.sum(
        weights[:, :, None]
        * expert_rows.reshape(tok_rows, top_count, width_model).astype(jnp.float32),
        axis=1,
    )
    return mixed.astype(jnp.bfloat16)


AXES = ("ez", "ex", "ec")


def gather_stage(block, axis, size):
    got = [block]
    for shift in range(1, size):
        pairs = [(i, (i + shift) % size) for i in range(size)]
        got.append(lax.ppermute(block, axis, pairs))
    return jnp.concatenate(got, axis=0)


def scatter_stage(part, axis, size):
    pieces = jnp.split(part, size, axis=0)
    total = pieces[0].astype(jnp.float32)
    for shift in range(1, size):
        pairs = [(i, (i - shift) % size) for i in range(size)]
        total = total + lax.ppermute(pieces[shift].astype(jnp.bfloat16), axis, pairs).astype(jnp.float32)
    return total


def dense_shards(tokens, expert_ids, gate_scores, host_expert, w_in, w_down):
    tok_rows, width_model = tokens.shape
    hidden_width = w_down.shape[1]
    experts = host_expert.shape[0]
    sizes = [lax.axis_size(a) for a in AXES]
    hosts = sizes[0] * sizes[1] * sizes[2]
    me = (lax.axis_index("ez") * sizes[1] + lax.axis_index("ex")) * sizes[2] + lax.axis_index("ec")
    weights = gate_scores / jnp.sum(gate_scores, axis=1, keepdims=True)
    chosen = expert_ids[:, :, None] == host_expert[None, None, :]
    per_host = jnp.sum(jnp.where(chosen, weights[:, :, None], 0.0), axis=1)
    hi = lax.reduce_precision(per_host, exponent_bits=8, mantissa_bits=7)
    rest = per_host - hi
    lo = lax.reduce_precision(rest, exponent_bits=8, mantissa_bits=7)
    lo2 = rest - lo
    extra = -(-3 * hosts // 128) * 128
    meta = jnp.concatenate([hi, lo, lo2, jnp.zeros((tok_rows, extra - 3 * hosts), jnp.float32)], axis=1)
    meta = meta.astype(jnp.bfloat16)
    carried = jnp.concatenate([tokens, meta], axis=1)
    pick = (jnp.arange(hosts, dtype=jnp.int32) == me).astype(jnp.float32)
    results = []
    held = None
    for rows in jnp.split(carried, STREAMS, axis=0):
        if held is not None:
            held, rows = lax.optimization_barrier((held, rows))
        rows = gather_stage(rows, AXES[0], sizes[0])
        held = rows
        for axis, size in zip(AXES[1:], sizes[1:]):
            rows = gather_stage(rows, axis, size)
        tail = rows[:, width_model:width_model + 3 * hosts].astype(jnp.float32)
        gate = tail[:, :hosts] + tail[:, hosts:2 * hosts] + tail[:, 2 * hosts:]
        mine = jnp.sum(gate * pick[None, :], axis=1)
        out = expert_block(rows[:, :width_model], w_in[0], w_down[0], hidden_width)
        part = out.astype(jnp.float32) * mine[:, None]
        for axis, size in list(zip(AXES, sizes))[::-1]:
            part = scatter_stage(part, axis, size)
        results.append(part)
    return jnp.concatenate(results, axis=0).astype(jnp.bfloat16)


STREAMS = 4


def factor_expert(mesh):
    row = mesh.devices[0]
    try:
        cores = len({d.core_on_chip for d in row})
        xs = len({d.coords[0] for d in row})
        zs = len({d.coords[2] for d in row})
    except AttributeError:
        return None
    if cores * xs * zs != row.shape[0]:
        return None
    return zs, xs, cores


def solution(mesh):
    placed = (
        P(("groups", "expert"), None),
        P(("groups", "expert"), None),
        P(("groups", "expert"), None),
        P(),
        P("expert", None, None),
        P("expert", None, None),
    )
    factors = factor_expert(mesh)
    if factors is None or mesh.shape["expert"] > 16:
        return jax.shard_map(
            shards, mesh=mesh, in_specs=placed, out_specs=P(("groups", "expert"), None), check_vma=False
        )
    sub = Mesh(mesh.devices.reshape((mesh.shape["groups"],) + factors), ("groups",) + AXES)
    rows = P(("groups",) + AXES, None)
    placed = (rows, rows, rows, P(), P(AXES, None, None), P(AXES, None, None))
    return jax.shard_map(dense_shards, mesh=sub, in_specs=placed, out_specs=rows, check_vma=False)
```

```python
import jax
import jax.numpy as jnp
import numpy as np
from jax import lax
from jax.sharding import Mesh, PartitionSpec as P


def expert_block(rows_in, gate_up, down_proj, hidden_width):
    pair = jnp.dot(rows_in, gate_up, preferred_element_type=jnp.float32)
    active = (jax.nn.silu(pair[:, :hidden_width]) * pair[:, hidden_width:]).astype(jnp.bfloat16)
    return jnp.dot(active, down_proj, preferred_element_type=jnp.float32).astype(jnp.bfloat16)


def shards(tokens, expert_ids, gate_scores, host_expert, w_in, w_down):
    tok_rows, width_model = tokens.shape
    top_count = expert_ids.shape[1]
    hosts = lax.axis_size("expert")
    experts = host_expert.shape[0]
    capacity = 3 * tok_rows * top_count // (2 * experts)
    hidden_width = w_down.shape[1]
    routed = tok_rows * top_count
    slots = hosts * capacity
    gate_up = w_in[0]
    down_proj = w_down[0]
    expert_range = jnp.arange(experts, dtype=jnp.int32)
    host_range = jnp.arange(hosts, dtype=jnp.int32)
    placed = (host_expert[:, None] == expert_range[None, :]).astype(jnp.int32)
    host_of = jnp.sum(placed * host_range[:, None], axis=0)
    flat_ids = expert_ids.reshape(-1)
    id_match = flat_ids[:, None] == expert_range[None, :]
    dest_host = jnp.sum(jnp.where(id_match, host_of[None, :], 0), axis=1)
    row_token = jnp.arange(routed, dtype=jnp.int32) // top_count
    padded_tokens = jnp.concatenate([tokens, jnp.zeros((1, width_model), tokens.dtype)], axis=0)
    earlier = (
        lax.broadcasted_iota(jnp.int32, (routed, routed), 0)
        > lax.broadcasted_iota(jnp.int32, (routed, routed), 1)
    ).astype(jnp.bfloat16)
    dest_match = dest_host[:, None] == host_range[None, :]
    before = jnp.dot(earlier, dest_match.astype(jnp.bfloat16), preferred_element_type=jnp.float32)
    position = jnp.sum(jnp.where(dest_match, before, 0.0), axis=1).astype(jnp.int32)
    slot_of_row = dest_host * capacity + position
    source_row = jnp.full((slots + 1,), tok_rows, jnp.int32).at[slot_of_row].set(row_token)[:slots]
    outgoing = padded_tokens[source_row].reshape(hosts, capacity, width_model)
    received = lax.all_to_all(outgoing, "expert", split_axis=0, concat_axis=0, tiled=True)
    flat_in = received.reshape(-1, width_model)
    served = expert_block(flat_in, gate_up, down_proj, hidden_width).reshape(received.shape)
    returned = lax.all_to_all(served, "expert", split_axis=0, concat_axis=0, tiled=True)
    expert_rows = returned.reshape(slots, width_model)[slot_of_row]
    weights = gate_scores / jnp.sum(gate_scores, axis=1, keepdims=True)
    mixed = jnp.sum(
        weights[:, :, None]
        * expert_rows.reshape(tok_rows, top_count, width_model).astype(jnp.float32),
        axis=1,
    )
    return mixed.astype(jnp.bfloat16)


AXES = ("ez", "ex", "ec")


def gather_stage(block, axis, size):
    if size > 2:
        spread = jnp.broadcast_to(block[None], (size,) + block.shape)
        return lax.all_to_all(spread, axis, 0, 0, tiled=True).reshape((-1,) + block.shape[1:])
    got = [block]
    for shift in range(1, size):
        pairs = [(i, (i + shift) % size) for i in range(size)]
        got.append(lax.ppermute(block, axis, pairs))
    return jnp.concatenate(got, axis=0)


def scatter_stage(part, axis, size):
    if size > 2:
        sent = part.astype(jnp.bfloat16).reshape((size, -1) + part.shape[1:])
        back = lax.all_to_all(sent, axis, 0, 0, tiled=True)
        return jnp.sum(back.astype(jnp.float32), axis=0)
    pieces = jnp.split(part, size, axis=0)
    total = pieces[0].astype(jnp.float32)
    for shift in range(1, size):
        pairs = [(i, (i - shift) % size) for i in range(size)]
        total = total + lax.ppermute(pieces[shift].astype(jnp.bfloat16), axis, pairs).astype(jnp.float32)
    return total


def dense_shards(tokens, expert_ids, gate_scores, host_expert, w_in, w_down):
    tok_rows, width_model = tokens.shape
    hidden_width = w_down.shape[1]
    experts = host_expert.shape[0]
    sizes = [lax.axis_size(a) for a in AXES]
    hosts = sizes[0] * sizes[1] * sizes[2]
    me = (lax.axis_index("ez") * sizes[1] + lax.axis_index("ex")) * sizes[2] + lax.axis_index("ec")
    weights = gate_scores / jnp.sum(gate_scores, axis=1, keepdims=True)
    chosen = expert_ids[:, :, None] == host_expert[None, None, :]
    per_host = jnp.sum(jnp.where(chosen, weights[:, :, None], 0.0), axis=1)
    hi = lax.reduce_precision(per_host, exponent_bits=8, mantissa_bits=7)
    rest = per_host - hi
    lo = lax.reduce_precision(rest, exponent_bits=8, mantissa_bits=7)
    lo2 = rest - lo
    extra = -(-3 * hosts // 128) * 128
    meta = jnp.concatenate([hi, lo, lo2, jnp.zeros((tok_rows, extra - 3 * hosts), jnp.float32)], axis=1)
    meta = meta.astype(jnp.bfloat16)
    carried = jnp.concatenate([tokens, meta], axis=1)
    pick = (jnp.arange(hosts, dtype=jnp.int32) == me).astype(jnp.float32)
    results = []
    held = None
    for rows in jnp.split(carried, STREAMS, axis=0):
        if held is not None:
            held, rows = lax.optimization_barrier((held, rows))
        rows = gather_stage(rows, AXES[0], sizes[0])
        held = rows
        for axis, size in zip(AXES[1:], sizes[1:]):
            rows = gather_stage(rows, axis, size)
        tail = rows[:, width_model:width_model + 3 * hosts].astype(jnp.float32)
        gate = tail[:, :hosts] + tail[:, hosts:2 * hosts] + tail[:, 2 * hosts:]
        mine = jnp.sum(gate * pick[None, :], axis=1)
        out = expert_block(rows[:, :width_model], w_in[0], w_down[0], hidden_width)
        part = out.astype(jnp.float32) * mine[:, None]
        for axis, size in list(zip(AXES, sizes))[::-1]:
            part = scatter_stage(part, axis, size)
        results.append(part)
    return jnp.concatenate(results, axis=0).astype(jnp.bfloat16)


STREAMS = 2


def factor_expert(mesh):
    row = mesh.devices[0]
    try:
        cores = len({d.core_on_chip for d in row})
        xs = len({d.coords[0] for d in row})
        zs = len({d.coords[2] for d in row})
    except AttributeError:
        return None
    if cores * xs * zs != row.shape[0]:
        return None
    return zs, xs, cores


def solution(mesh):
    placed = (
        P(("groups", "expert"), None),
        P(("groups", "expert"), None),
        P(("groups", "expert"), None),
        P(),
        P("expert", None, None),
        P("expert", None, None),
    )
    factors = factor_expert(mesh)
    if factors is None or mesh.shape["expert"] > 16:
        return jax.shard_map(
            shards, mesh=mesh, in_specs=placed, out_specs=P(("groups", "expert"), None), check_vma=False
        )
    sub = Mesh(mesh.devices.reshape((mesh.shape["groups"],) + factors), ("groups",) + AXES)
    rows = P(("groups",) + AXES, None)
    placed = (rows, rows, rows, P(), P(AXES, None, None), P(AXES, None, None))
    return jax.shard_map(dense_shards, mesh=sub, in_specs=placed, out_specs=rows, check_vma=False)
```

```python
import jax
import jax.numpy as jnp
import numpy as np
from jax import lax
from jax.sharding import Mesh, PartitionSpec as P


def expert_block(rows_in, gate_up, down_proj, hidden_width):
    pair = jnp.dot(rows_in, gate_up, preferred_element_type=jnp.float32)
    active = (jax.nn.silu(pair[:, :hidden_width]) * pair[:, hidden_width:]).astype(jnp.bfloat16)
    return jnp.dot(active, down_proj, preferred_element_type=jnp.float32).astype(jnp.bfloat16)


def shards(tokens, expert_ids, gate_scores, host_expert, w_in, w_down):
    tok_rows, width_model = tokens.shape
    top_count = expert_ids.shape[1]
    hosts = lax.axis_size("expert")
    experts = host_expert.shape[0]
    capacity = 3 * tok_rows * top_count // (2 * experts)
    hidden_width = w_down.shape[1]
    routed = tok_rows * top_count
    slots = hosts * capacity
    gate_up = w_in[0]
    down_proj = w_down[0]
    expert_range = jnp.arange(experts, dtype=jnp.int32)
    host_range = jnp.arange(hosts, dtype=jnp.int32)
    placed = (host_expert[:, None] == expert_range[None, :]).astype(jnp.int32)
    host_of = jnp.sum(placed * host_range[:, None], axis=0)
    flat_ids = expert_ids.reshape(-1)
    id_match = flat_ids[:, None] == expert_range[None, :]
    dest_host = jnp.sum(jnp.where(id_match, host_of[None, :], 0), axis=1)
    row_token = jnp.arange(routed, dtype=jnp.int32) // top_count
    padded_tokens = jnp.concatenate([tokens, jnp.zeros((1, width_model), tokens.dtype)], axis=0)
    earlier = (
        lax.broadcasted_iota(jnp.int32, (routed, routed), 0)
        > lax.broadcasted_iota(jnp.int32, (routed, routed), 1)
    ).astype(jnp.bfloat16)
    dest_match = dest_host[:, None] == host_range[None, :]
    before = jnp.dot(earlier, dest_match.astype(jnp.bfloat16), preferred_element_type=jnp.float32)
    position = jnp.sum(jnp.where(dest_match, before, 0.0), axis=1).astype(jnp.int32)
    slot_of_row = dest_host * capacity + position
    source_row = jnp.full((slots + 1,), tok_rows, jnp.int32).at[slot_of_row].set(row_token)[:slots]
    outgoing = padded_tokens[source_row].reshape(hosts, capacity, width_model)
    received = lax.all_to_all(outgoing, "expert", split_axis=0, concat_axis=0, tiled=True)
    flat_in = received.reshape(-1, width_model)
    served = expert_block(flat_in, gate_up, down_proj, hidden_width).reshape(received.shape)
    returned = lax.all_to_all(served, "expert", split_axis=0, concat_axis=0, tiled=True)
    expert_rows = returned.reshape(slots, width_model)[slot_of_row]
    weights = gate_scores / jnp.sum(gate_scores, axis=1, keepdims=True)
    mixed = jnp.sum(
        weights[:, :, None]
        * expert_rows.reshape(tok_rows, top_count, width_model).astype(jnp.float32),
        axis=1,
    )
    return mixed.astype(jnp.bfloat16)


AXES = ("ez", "ex", "ec")


def gather_stage(block, axis, size):
    got = [block]
    for shift in range(1, size):
        pairs = [(i, (i + shift) % size) for i in range(size)]
        got.append(lax.ppermute(block, axis, pairs))
    return jnp.concatenate(got, axis=0)


def scatter_stage(part, axis, size):
    pieces = jnp.split(part, size, axis=0)
    total = pieces[0].astype(jnp.float32)
    for shift in range(1, size):
        pairs = [(i, (i - shift) % size) for i in range(size)]
        total = total + lax.ppermute(pieces[shift].astype(jnp.bfloat16), axis, pairs).astype(jnp.float32)
    return total


def dense_shards(tokens, expert_ids, gate_scores, host_expert, w_in, w_down):
    tok_rows, width_model = tokens.shape
    hidden_width = w_down.shape[1]
    experts = host_expert.shape[0]
    sizes = [lax.axis_size(a) for a in AXES]
    hosts = sizes[0] * sizes[1] * sizes[2]
    me = (lax.axis_index("ez") * sizes[1] + lax.axis_index("ex")) * sizes[2] + lax.axis_index("ec")
    weights = gate_scores / jnp.sum(gate_scores, axis=1, keepdims=True)
    chosen = expert_ids[:, :, None] == host_expert[None, None, :]
    per_host = jnp.sum(jnp.where(chosen, weights[:, :, None], 0.0), axis=1)
    hi = lax.reduce_precision(per_host, exponent_bits=8, mantissa_bits=7)
    rest = per_host - hi
    lo = lax.reduce_precision(rest, exponent_bits=8, mantissa_bits=7)
    lo2 = rest - lo
    extra = -(-3 * hosts // 128) * 128
    meta = jnp.concatenate([hi, lo, lo2, jnp.zeros((tok_rows, extra - 3 * hosts), jnp.float32)], axis=1)
    meta = meta.astype(jnp.bfloat16)
    carried = jnp.concatenate([tokens, meta], axis=1)
    pick = (jnp.arange(hosts, dtype=jnp.int32) == me).astype(jnp.float32)
    results = []
    held = None
    for rows in jnp.split(carried, STREAMS, axis=0):
        done = []
        for stage, (axis, size) in enumerate(zip(AXES, sizes)):
            if held is not None:
                _, rows = lax.optimization_barrier((held[(0, 2, 3)[stage]], rows))
            rows = gather_stage(rows, axis, size)
            done.append(rows)
        tail = rows[:, width_model:width_model + 3 * hosts].astype(jnp.float32)
        gate = tail[:, :hosts] + tail[:, hosts:2 * hosts] + tail[:, 2 * hosts:]
        mine = jnp.sum(gate * pick[None, :], axis=1)
        out = expert_block(rows[:, :width_model], w_in[0], w_down[0], hidden_width)
        held = done + [out]
        part = out.astype(jnp.float32) * mine[:, None]
        for axis, size in list(zip(AXES, sizes))[::-1]:
            part = scatter_stage(part, axis, size)
        results.append(part)
    return jnp.concatenate(results, axis=0).astype(jnp.bfloat16)


STREAMS = 2


def factor_expert(mesh):
    row = mesh.devices[0]
    try:
        cores = len({d.core_on_chip for d in row})
        xs = len({d.coords[0] for d in row})
        zs = len({d.coords[2] for d in row})
    except AttributeError:
        return None
    if cores * xs * zs != row.shape[0]:
        return None
    return zs, xs, cores


def solution(mesh):
    placed = (
        P(("groups", "expert"), None),
        P(("groups", "expert"), None),
        P(("groups", "expert"), None),
        P(),
        P("expert", None, None),
        P("expert", None, None),
    )
    factors = factor_expert(mesh)
    if factors is None or mesh.shape["expert"] > 16:
        return jax.shard_map(
            shards, mesh=mesh, in_specs=placed, out_specs=P(("groups", "expert"), None), check_vma=False
        )
    sub = Mesh(mesh.devices.reshape((mesh.shape["groups"],) + factors), ("groups",) + AXES)
    rows = P(("groups",) + AXES, None)
    placed = (rows, rows, rows, P(), P(AXES, None, None), P(AXES, None, None))
    return jax.shard_map(dense_shards, mesh=sub, in_specs=placed, out_specs=rows, check_vma=False)
```

```python
import jax
import jax.numpy as jnp
import numpy as np
from jax import lax
from jax.sharding import Mesh, PartitionSpec as P


def expert_block(rows_in, gate_up, down_proj, hidden_width):
    pair = jnp.dot(rows_in, gate_up, preferred_element_type=jnp.float32)
    active = (jax.nn.silu(pair[:, :hidden_width]) * pair[:, hidden_width:]).astype(jnp.bfloat16)
    return jnp.dot(active, down_proj, preferred_element_type=jnp.float32).astype(jnp.bfloat16)


def shards(tokens, expert_ids, gate_scores, host_expert, w_in, w_down):
    tok_rows, width_model = tokens.shape
    top_count = expert_ids.shape[1]
    hosts = lax.axis_size("expert")
    experts = host_expert.shape[0]
    capacity = 3 * tok_rows * top_count // (2 * experts)
    hidden_width = w_down.shape[1]
    routed = tok_rows * top_count
    slots = hosts * capacity
    gate_up = w_in[0]
    down_proj = w_down[0]
    expert_range = jnp.arange(experts, dtype=jnp.int32)
    host_range = jnp.arange(hosts, dtype=jnp.int32)
    placed = (host_expert[:, None] == expert_range[None, :]).astype(jnp.int32)
    host_of = jnp.sum(placed * host_range[:, None], axis=0)
    flat_ids = expert_ids.reshape(-1)
    id_match = flat_ids[:, None] == expert_range[None, :]
    dest_host = jnp.sum(jnp.where(id_match, host_of[None, :], 0), axis=1)
    row_token = jnp.arange(routed, dtype=jnp.int32) // top_count
    padded_tokens = jnp.concatenate([tokens, jnp.zeros((1, width_model), tokens.dtype)], axis=0)
    earlier = (
        lax.broadcasted_iota(jnp.int32, (routed, routed), 0)
        > lax.broadcasted_iota(jnp.int32, (routed, routed), 1)
    ).astype(jnp.bfloat16)
    dest_match = dest_host[:, None] == host_range[None, :]
    before = jnp.dot(earlier, dest_match.astype(jnp.bfloat16), preferred_element_type=jnp.float32)
    position = jnp.sum(jnp.where(dest_match, before, 0.0), axis=1).astype(jnp.int32)
    slot_of_row = dest_host * capacity + position
    source_row = jnp.full((slots + 1,), tok_rows, jnp.int32).at[slot_of_row].set(row_token)[:slots]
    outgoing = padded_tokens[source_row].reshape(hosts, capacity, width_model)
    received = lax.all_to_all(outgoing, "expert", split_axis=0, concat_axis=0, tiled=True)
    flat_in = received.reshape(-1, width_model)
    served = expert_block(flat_in, gate_up, down_proj, hidden_width).reshape(received.shape)
    returned = lax.all_to_all(served, "expert", split_axis=0, concat_axis=0, tiled=True)
    expert_rows = returned.reshape(slots, width_model)[slot_of_row]
    weights = gate_scores / jnp.sum(gate_scores, axis=1, keepdims=True)
    mixed = jnp.sum(
        weights[:, :, None]
        * expert_rows.reshape(tok_rows, top_count, width_model).astype(jnp.float32),
        axis=1,
    )
    return mixed.astype(jnp.bfloat16)


AXES = ("ezh", "ezl", "ex", "ec")


def gather_stage(block, axis, size):
    got = [block]
    for shift in range(1, size):
        pairs = [(i, (i + shift) % size) for i in range(size)]
        got.append(lax.ppermute(block, axis, pairs))
    return jnp.concatenate(got, axis=0)


def scatter_stage(part, axis, size):
    pieces = jnp.split(part, size, axis=0)
    total = pieces[0].astype(jnp.float32)
    for shift in range(1, size):
        pairs = [(i, (i - shift) % size) for i in range(size)]
        total = total + lax.ppermute(pieces[shift].astype(jnp.bfloat16), axis, pairs).astype(jnp.float32)
    return total


def dense_shards(tokens, expert_ids, gate_scores, host_expert, w_in, w_down):
    tok_rows, width_model = tokens.shape
    hidden_width = w_down.shape[1]
    experts = host_expert.shape[0]
    sizes = [lax.axis_size(a) for a in AXES]
    hosts = int(np.prod(sizes))
    me = 0
    for axis, size in zip(AXES, sizes):
        me = me * size + lax.axis_index(axis)
    weights = gate_scores / jnp.sum(gate_scores, axis=1, keepdims=True)
    chosen = expert_ids[:, :, None] == host_expert[None, None, :]
    per_host = jnp.sum(jnp.where(chosen, weights[:, :, None], 0.0), axis=1)
    hi = lax.reduce_precision(per_host, exponent_bits=8, mantissa_bits=7)
    rest = per_host - hi
    lo = lax.reduce_precision(rest, exponent_bits=8, mantissa_bits=7)
    lo2 = rest - lo
    extra = -(-3 * hosts // 128) * 128
    meta = jnp.concatenate([hi, lo, lo2, jnp.zeros((tok_rows, extra - 3 * hosts), jnp.float32)], axis=1)
    meta = meta.astype(jnp.bfloat16)
    carried = jnp.concatenate([tokens, meta], axis=1)
    pick = (jnp.arange(hosts, dtype=jnp.int32) == me).astype(jnp.float32)
    results = []
    held = None
    for rows in jnp.split(carried, STREAMS, axis=0):
        if held is not None:
            held, rows = lax.optimization_barrier((held, rows))
        rows = gather_stage(rows, AXES[0], sizes[0])
        held = rows
        for axis, size in zip(AXES[1:], sizes[1:]):
            rows = gather_stage(rows, axis, size)
        tail = rows[:, width_model:width_model + 3 * hosts].astype(jnp.float32)
        gate = tail[:, :hosts] + tail[:, hosts:2 * hosts] + tail[:, 2 * hosts:]
        mine = jnp.sum(gate * pick[None, :], axis=1)
        out = expert_block(rows[:, :width_model], w_in[0], w_down[0], hidden_width)
        part = out.astype(jnp.float32) * mine[:, None]
        for axis, size in list(zip(AXES, sizes))[::-1]:
            part = scatter_stage(part, axis, size)
        results.append(part)
    return jnp.concatenate(results, axis=0).astype(jnp.bfloat16)


STREAMS = 2


def factor_expert(mesh):
    row = mesh.devices[0]
    try:
        cores = len({d.core_on_chip for d in row})
        xs = len({d.coords[0] for d in row})
        zs = len({d.coords[2] for d in row})
    except AttributeError:
        return None
    if cores * xs * zs != row.shape[0] or zs % 2:
        return None
    return zs // 2, 2, xs, cores


def solution(mesh):
    placed = (
        P(("groups", "expert"), None),
        P(("groups", "expert"), None),
        P(("groups", "expert"), None),
        P(),
        P("expert", None, None),
        P("expert", None, None),
    )
    factors = factor_expert(mesh)
    if factors is None or mesh.shape["expert"] > 16:
        return jax.shard_map(
            shards, mesh=mesh, in_specs=placed, out_specs=P(("groups", "expert"), None), check_vma=False
        )
    sub = Mesh(mesh.devices.reshape((mesh.shape["groups"],) + factors), ("groups",) + AXES)
    rows = P(("groups",) + AXES, None)
    placed = (rows, rows, rows, P(), P(AXES, None, None), P(AXES, None, None))
    return jax.shard_map(dense_shards, mesh=sub, in_specs=placed, out_specs=rows, check_vma=False)
```

```python
import jax
import jax.numpy as jnp
import numpy as np
from jax import lax
from jax.sharding import Mesh, PartitionSpec as P


def expert_block(rows_in, gate_up, down_proj, hidden_width):
    pair = jnp.dot(rows_in, gate_up, preferred_element_type=jnp.float32)
    active = (jax.nn.silu(pair[:, :hidden_width]) * pair[:, hidden_width:]).astype(jnp.bfloat16)
    return jnp.dot(active, down_proj, preferred_element_type=jnp.float32).astype(jnp.bfloat16)


def shards(tokens, expert_ids, gate_scores, host_expert, w_in, w_down):
    tok_rows, width_model = tokens.shape
    top_count = expert_ids.shape[1]
    hosts = lax.axis_size("expert")
    experts = host_expert.shape[0]
    capacity = 3 * tok_rows * top_count // (2 * experts)
    hidden_width = w_down.shape[1]
    routed = tok_rows * top_count
    slots = hosts * capacity
    gate_up = w_in[0]
    down_proj = w_down[0]
    expert_range = jnp.arange(experts, dtype=jnp.int32)
    host_range = jnp.arange(hosts, dtype=jnp.int32)
    placed = (host_expert[:, None] == expert_range[None, :]).astype(jnp.int32)
    host_of = jnp.sum(placed * host_range[:, None], axis=0)
    flat_ids = expert_ids.reshape(-1)
    id_match = flat_ids[:, None] == expert_range[None, :]
    dest_host = jnp.sum(jnp.where(id_match, host_of[None, :], 0), axis=1)
    row_token = jnp.arange(routed, dtype=jnp.int32) // top_count
    padded_tokens = jnp.concatenate([tokens, jnp.zeros((1, width_model), tokens.dtype)], axis=0)
    earlier = (
        lax.broadcasted_iota(jnp.int32, (routed, routed), 0)
        > lax.broadcasted_iota(jnp.int32, (routed, routed), 1)
    ).astype(jnp.bfloat16)
    dest_match = dest_host[:, None] == host_range[None, :]
    before = jnp.dot(earlier, dest_match.astype(jnp.bfloat16), preferred_element_type=jnp.float32)
    position = jnp.sum(jnp.where(dest_match, before, 0.0), axis=1).astype(jnp.int32)
    slot_of_row = dest_host * capacity + position
    source_row = jnp.full((slots + 1,), tok_rows, jnp.int32).at[slot_of_row].set(row_token)[:slots]
    outgoing = padded_tokens[source_row].reshape(hosts, capacity, width_model)
    received = lax.all_to_all(outgoing, "expert", split_axis=0, concat_axis=0, tiled=True)
    flat_in = received.reshape(-1, width_model)
    served = expert_block(flat_in, gate_up, down_proj, hidden_width).reshape(received.shape)
    returned = lax.all_to_all(served, "expert", split_axis=0, concat_axis=0, tiled=True)
    expert_rows = returned.reshape(slots, width_model)[slot_of_row]
    weights = gate_scores / jnp.sum(gate_scores, axis=1, keepdims=True)
    mixed = jnp.sum(
        weights[:, :, None]
        * expert_rows.reshape(tok_rows, top_count, width_model).astype(jnp.float32),
        axis=1,
    )
    return mixed.astype(jnp.bfloat16)


AXES = ("ez", "ex", "ec")


def gather_stage(block, axis, size):
    got = [block]
    for shift in range(1, size):
        pairs = [(i, (i + shift) % size) for i in range(size)]
        got.append(lax.ppermute(block, axis, pairs))
    return jnp.concatenate(got, axis=0)


def scatter_stage(part, axis, size):
    pieces = jnp.split(part, size, axis=0)
    total = pieces[0].astype(jnp.float32)
    for shift in range(1, size):
        pairs = [(i, (i - shift) % size) for i in range(size)]
        total = total + lax.ppermute(pieces[shift].astype(jnp.bfloat16), axis, pairs).astype(jnp.float32)
    return total


def dense_shards(tokens, expert_ids, gate_scores, host_expert, w_in, w_down):
    tok_rows, width_model = tokens.shape
    hidden_width = w_down.shape[1]
    experts = host_expert.shape[0]
    sizes = [lax.axis_size(a) for a in AXES]
    hosts = sizes[0] * sizes[1] * sizes[2]
    me = (lax.axis_index("ez") * sizes[1] + lax.axis_index("ex")) * sizes[2] + lax.axis_index("ec")
    weights = gate_scores / jnp.sum(gate_scores, axis=1, keepdims=True)
    chosen = expert_ids[:, :, None] == host_expert[None, None, :]
    per_host = jnp.sum(jnp.where(chosen, weights[:, :, None], 0.0), axis=1)
    hi = lax.reduce_precision(per_host, exponent_bits=8, mantissa_bits=7)
    rest = per_host - hi
    lo = lax.reduce_precision(rest, exponent_bits=8, mantissa_bits=7)
    lo2 = rest - lo
    extra = -(-3 * hosts // 128) * 128
    meta = jnp.concatenate([hi, lo, lo2, jnp.zeros((tok_rows, extra - 3 * hosts), jnp.float32)], axis=1)
    meta = meta.astype(jnp.bfloat16)
    carried = jnp.concatenate([tokens, meta], axis=1)
    pick = (jnp.arange(hosts, dtype=jnp.int32) == me).astype(jnp.float32)
    results = []
    held = None
    for rows in jnp.split(carried, STREAMS, axis=0):
        done = [None] * (2 * len(AXES))
        for stage, (axis, size) in enumerate(zip(AXES, sizes)):
            if held is not None:
                _, rows = lax.optimization_barrier((held[stage], rows))
            rows = gather_stage(rows, axis, size)
            done[stage] = rows
        tail = rows[:, width_model:width_model + 3 * hosts].astype(jnp.float32)
        gate = tail[:, :hosts] + tail[:, hosts:2 * hosts] + tail[:, 2 * hosts:]
        mine = jnp.sum(gate * pick[None, :], axis=1)
        out = expert_block(rows[:, :width_model], w_in[0], w_down[0], hidden_width)
        part = out.astype(jnp.float32) * mine[:, None]
        for stage, (axis, size) in list(enumerate(zip(AXES, sizes)))[::-1]:
            if held is not None:
                _, part = lax.optimization_barrier((held[len(AXES) + stage], part))
            part = scatter_stage(part, axis, size)
            done[len(AXES) + stage] = part
        held = done
        results.append(part)
    return jnp.concatenate(results, axis=0).astype(jnp.bfloat16)


STREAMS = 2


def factor_expert(mesh):
    row = mesh.devices[0]
    try:
        cores = len({d.core_on_chip for d in row})
        xs = len({d.coords[0] for d in row})
        zs = len({d.coords[2] for d in row})
    except AttributeError:
        return None
    if cores * xs * zs != row.shape[0]:
        return None
    return zs, xs, cores


def solution(mesh):
    placed = (
        P(("groups", "expert"), None),
        P(("groups", "expert"), None),
        P(("groups", "expert"), None),
        P(),
        P("expert", None, None),
        P("expert", None, None),
    )
    factors = factor_expert(mesh)
    if factors is None or mesh.shape["expert"] > 16:
        return jax.shard_map(
            shards, mesh=mesh, in_specs=placed, out_specs=P(("groups", "expert"), None), check_vma=False
        )
    sub = Mesh(mesh.devices.reshape((mesh.shape["groups"],) + factors), ("groups",) + AXES)
    rows = P(("groups",) + AXES, None)
    placed = (rows, rows, rows, P(), P(AXES, None, None), P(AXES, None, None))
    return jax.shard_map(dense_shards, mesh=sub, in_specs=placed, out_specs=rows, check_vma=False)
```

```python
import jax
import jax.numpy as jnp
import numpy as np
from jax import lax
from jax.sharding import Mesh, PartitionSpec as P


def expert_block(rows_in, gate_up, down_proj, hidden_width):
    pair = jnp.dot(rows_in, gate_up, preferred_element_type=jnp.float32)
    active = (jax.nn.silu(pair[:, :hidden_width]) * pair[:, hidden_width:]).astype(jnp.bfloat16)
    return jnp.dot(active, down_proj, preferred_element_type=jnp.float32).astype(jnp.bfloat16)


def shards(tokens, expert_ids, gate_scores, host_expert, w_in, w_down):
    tok_rows, width_model = tokens.shape
    top_count = expert_ids.shape[1]
    hosts = lax.axis_size("expert")
    experts = host_expert.shape[0]
    capacity = 3 * tok_rows * top_count // (2 * experts)
    hidden_width = w_down.shape[1]
    routed = tok_rows * top_count
    slots = hosts * capacity
    gate_up = w_in[0]
    down_proj = w_down[0]
    expert_range = jnp.arange(experts, dtype=jnp.int32)
    host_range = jnp.arange(hosts, dtype=jnp.int32)
    placed = (host_expert[:, None] == expert_range[None, :]).astype(jnp.int32)
    host_of = jnp.sum(placed * host_range[:, None], axis=0)
    flat_ids = expert_ids.reshape(-1)
    id_match = flat_ids[:, None] == expert_range[None, :]
    dest_host = jnp.sum(jnp.where(id_match, host_of[None, :], 0), axis=1)
    row_token = jnp.arange(routed, dtype=jnp.int32) // top_count
    padded_tokens = jnp.concatenate([tokens, jnp.zeros((1, width_model), tokens.dtype)], axis=0)
    earlier = (
        lax.broadcasted_iota(jnp.int32, (routed, routed), 0)
        > lax.broadcasted_iota(jnp.int32, (routed, routed), 1)
    ).astype(jnp.bfloat16)
    dest_match = dest_host[:, None] == host_range[None, :]
    before = jnp.dot(earlier, dest_match.astype(jnp.bfloat16), preferred_element_type=jnp.float32)
    position = jnp.sum(jnp.where(dest_match, before, 0.0), axis=1).astype(jnp.int32)
    slot_of_row = dest_host * capacity + position
    source_row = jnp.full((slots + 1,), tok_rows, jnp.int32).at[slot_of_row].set(row_token)[:slots]
    outgoing = padded_tokens[source_row].reshape(hosts, capacity, width_model)
    received = lax.all_to_all(outgoing, "expert", split_axis=0, concat_axis=0, tiled=True)
    flat_in = received.reshape(-1, width_model)
    served = expert_block(flat_in, gate_up, down_proj, hidden_width).reshape(received.shape)
    returned = lax.all_to_all(served, "expert", split_axis=0, concat_axis=0, tiled=True)
    expert_rows = returned.reshape(slots, width_model)[slot_of_row]
    weights = gate_scores / jnp.sum(gate_scores, axis=1, keepdims=True)
    mixed = jnp.sum(
        weights[:, :, None]
        * expert_rows.reshape(tok_rows, top_count, width_model).astype(jnp.float32),
        axis=1,
    )
    return mixed.astype(jnp.bfloat16)


AXES = ("ez", "ex", "ec")


def gather_stage(block, axis, size):
    got = [block]
    for shift in range(1, size):
        pairs = [(i, (i + shift) % size) for i in range(size)]
        got.append(lax.ppermute(block, axis, pairs))
    return jnp.concatenate(got, axis=0)


def scatter_stage(part, axis, size):
    pieces = jnp.split(part, size, axis=0)
    total = pieces[0].astype(jnp.float32)
    for shift in range(1, size):
        pairs = [(i, (i - shift) % size) for i in range(size)]
        total = total + lax.ppermute(pieces[shift].astype(jnp.bfloat16), axis, pairs).astype(jnp.float32)
    return total


def dense_shards(tokens, expert_ids, gate_scores, host_expert, w_in, w_down):
    tok_rows, width_model = tokens.shape
    hidden_width = w_down.shape[1]
    experts = host_expert.shape[0]
    sizes = [lax.axis_size(a) for a in AXES]
    hosts = sizes[0] * sizes[1] * sizes[2]
    me = (lax.axis_index("ez") * sizes[1] + lax.axis_index("ex")) * sizes[2] + lax.axis_index("ec")
    weights = gate_scores / jnp.sum(gate_scores, axis=1, keepdims=True)
    chosen = expert_ids[:, :, None] == host_expert[None, None, :]
    per_host = jnp.sum(jnp.where(chosen, weights[:, :, None], 0.0), axis=1)
    hi = lax.reduce_precision(per_host, exponent_bits=8, mantissa_bits=7)
    rest = per_host - hi
    lo = lax.reduce_precision(rest, exponent_bits=8, mantissa_bits=7)
    lo2 = rest - lo
    extra = -(-3 * hosts // 128) * 128
    meta = jnp.concatenate([hi, lo, lo2, jnp.zeros((tok_rows, extra - 3 * hosts), jnp.float32)], axis=1)
    meta = meta.astype(jnp.bfloat16)
    carried = jnp.concatenate([tokens, meta], axis=1)
    pick = (jnp.arange(hosts, dtype=jnp.int32) == me).astype(jnp.float32)
    results = []
    for rows in jnp.split(carried, STREAMS, axis=0):
        for axis, size in zip(AXES, sizes):
            rows = gather_stage(rows, axis, size)
        tail = rows[:, width_model:width_model + 3 * hosts].astype(jnp.float32)
        gate = tail[:, :hosts] + tail[:, hosts:2 * hosts] + tail[:, 2 * hosts:]
        mine = jnp.sum(gate * pick[None, :], axis=1)
        out = expert_block(rows[:, :width_model], w_in[0], w_down[0], hidden_width)
        part = out.astype(jnp.float32) * mine[:, None]
        for axis, size in list(zip(AXES, sizes))[::-1]:
            part = scatter_stage(part, axis, size)
        results.append(part)
    return jnp.concatenate(results, axis=0).astype(jnp.bfloat16)


STREAMS = 2


def factor_expert(mesh):
    row = mesh.devices[0]
    try:
        cores = len({d.core_on_chip for d in row})
        xs = len({d.coords[0] for d in row})
        zs = len({d.coords[2] for d in row})
    except AttributeError:
        return None
    if cores * xs * zs != row.shape[0]:
        return None
    return zs, xs, cores


def solution(mesh):
    placed = (
        P(("groups", "expert"), None),
        P(("groups", "expert"), None),
        P(("groups", "expert"), None),
        P(),
        P("expert", None, None),
        P("expert", None, None),
    )
    factors = factor_expert(mesh)
    if factors is None or mesh.shape["expert"] > 16:
        return jax.shard_map(
            shards, mesh=mesh, in_specs=placed, out_specs=P(("groups", "expert"), None), check_vma=False
        )
    sub = Mesh(mesh.devices.reshape((mesh.shape["groups"],) + factors), ("groups",) + AXES)
    rows = P(("groups",) + AXES, None)
    placed = (rows, rows, rows, P(), P(AXES, None, None), P(AXES, None, None))
    return jax.shard_map(dense_shards, mesh=sub, in_specs=placed, out_specs=rows, check_vma=False)
```

```python
import jax
import jax.numpy as jnp
import numpy as np
from jax import lax
from jax.sharding import Mesh, PartitionSpec as P


def expert_block(rows_in, gate_up, down_proj, hidden_width):
    pair = jnp.dot(rows_in, gate_up, preferred_element_type=jnp.float32)
    active = (jax.nn.silu(pair[:, :hidden_width]) * pair[:, hidden_width:]).astype(jnp.bfloat16)
    return jnp.dot(active, down_proj, preferred_element_type=jnp.float32).astype(jnp.bfloat16)


def shards(tokens, expert_ids, gate_scores, host_expert, w_in, w_down):
    tok_rows, width_model = tokens.shape
    top_count = expert_ids.shape[1]
    hosts = lax.axis_size("expert")
    experts = host_expert.shape[0]
    capacity = 3 * tok_rows * top_count // (2 * experts)
    hidden_width = w_down.shape[1]
    routed = tok_rows * top_count
    slots = hosts * capacity
    gate_up = w_in[0]
    down_proj = w_down[0]
    expert_range = jnp.arange(experts, dtype=jnp.int32)
    host_range = jnp.arange(hosts, dtype=jnp.int32)
    placed = (host_expert[:, None] == expert_range[None, :]).astype(jnp.int32)
    host_of = jnp.sum(placed * host_range[:, None], axis=0)
    flat_ids = expert_ids.reshape(-1)
    id_match = flat_ids[:, None] == expert_range[None, :]
    dest_host = jnp.sum(jnp.where(id_match, host_of[None, :], 0), axis=1)
    row_token = jnp.arange(routed, dtype=jnp.int32) // top_count
    padded_tokens = jnp.concatenate([tokens, jnp.zeros((1, width_model), tokens.dtype)], axis=0)
    earlier = (
        lax.broadcasted_iota(jnp.int32, (routed, routed), 0)
        > lax.broadcasted_iota(jnp.int32, (routed, routed), 1)
    ).astype(jnp.bfloat16)
    dest_match = dest_host[:, None] == host_range[None, :]
    before = jnp.dot(earlier, dest_match.astype(jnp.bfloat16), preferred_element_type=jnp.float32)
    position = jnp.sum(jnp.where(dest_match, before, 0.0), axis=1).astype(jnp.int32)
    slot_of_row = dest_host * capacity + position
    source_row = jnp.full((slots + 1,), tok_rows, jnp.int32).at[slot_of_row].set(row_token)[:slots]
    outgoing = padded_tokens[source_row].reshape(hosts, capacity, width_model)
    received = lax.all_to_all(outgoing, "expert", split_axis=0, concat_axis=0, tiled=True)
    flat_in = received.reshape(-1, width_model)
    served = expert_block(flat_in, gate_up, down_proj, hidden_width).reshape(received.shape)
    returned = lax.all_to_all(served, "expert", split_axis=0, concat_axis=0, tiled=True)
    expert_rows = returned.reshape(slots, width_model)[slot_of_row]
    weights = gate_scores / jnp.sum(gate_scores, axis=1, keepdims=True)
    mixed = jnp.sum(
        weights[:, :, None]
        * expert_rows.reshape(tok_rows, top_count, width_model).astype(jnp.float32),
        axis=1,
    )
    return mixed.astype(jnp.bfloat16)


AXES = ("ez", "ex", "ec")


def gather_stage(block, axis, size):
    got = [block]
    for shift in range(1, size):
        pairs = [(i, (i + shift) % size) for i in range(size)]
        got.append(lax.ppermute(block, axis, pairs))
    return jnp.concatenate(got, axis=0)


def scatter_stage(part, axis, size):
    pieces = jnp.split(part, size, axis=0)
    total = pieces[0].astype(jnp.float32)
    for shift in range(1, size):
        pairs = [(i, (i - shift) % size) for i in range(size)]
        total = total + lax.ppermute(pieces[shift].astype(jnp.bfloat16), axis, pairs).astype(jnp.float32)
    return total


def dense_shards(tokens, expert_ids, gate_scores, host_expert, w_in, w_down):
    tok_rows, width_model = tokens.shape
    hidden_width = w_down.shape[1]
    experts = host_expert.shape[0]
    sizes = [lax.axis_size(a) for a in AXES]
    hosts = sizes[0] * sizes[1] * sizes[2]
    me = (lax.axis_index("ez") * sizes[1] + lax.axis_index("ex")) * sizes[2] + lax.axis_index("ec")
    weights = gate_scores / jnp.sum(gate_scores, axis=1, keepdims=True)
    chosen = expert_ids[:, :, None] == host_expert[None, None, :]
    per_host = jnp.sum(jnp.where(chosen, weights[:, :, None], 0.0), axis=1)
    hi = lax.reduce_precision(per_host, exponent_bits=8, mantissa_bits=7)
    rest = per_host - hi
    lo = lax.reduce_precision(rest, exponent_bits=8, mantissa_bits=7)
    lo2 = rest - lo
    extra = -(-3 * hosts // 128) * 128
    meta = jnp.concatenate([hi, lo, lo2, jnp.zeros((tok_rows, extra - 3 * hosts), jnp.float32)], axis=1)
    meta = meta.astype(jnp.bfloat16)
    carried = jnp.concatenate([tokens, meta], axis=1)
    pick = (jnp.arange(hosts, dtype=jnp.int32) == me).astype(jnp.float32)
    z_blocks = [carried] + [
        lax.ppermute(carried, AXES[0], [(i, (i + shift) % sizes[0]) for i in range(sizes[0])])
        for shift in range(1, sizes[0])
    ]
    swap = [(i, (i + 1) % sizes[1]) for i in range(sizes[1])]
    x_blocks = [lax.ppermute(block, AXES[1], swap) for block in z_blocks]
    rows = jnp.concatenate(z_blocks + x_blocks, axis=0)
    rows = gather_stage(rows, AXES[2], sizes[2])
    tail = rows[:, width_model:width_model + 3 * hosts].astype(jnp.float32)
    gate = tail[:, :hosts] + tail[:, hosts:2 * hosts] + tail[:, 2 * hosts:]
    mine = jnp.sum(gate * pick[None, :], axis=1)
    out = expert_block(rows[:, :width_model], w_in[0], w_down[0], hidden_width)
    part = out.astype(jnp.float32) * mine[:, None]
    part = scatter_stage(part, AXES[2], sizes[2])
    own, other = jnp.split(part, 2, axis=0)
    own_blocks = jnp.split(own, sizes[0], axis=0)
    other_blocks = jnp.split(other, sizes[0], axis=0)
    total = None
    for shift in range(sizes[0]):
        block = own_blocks[shift] + lax.ppermute(
            other_blocks[shift].astype(jnp.bfloat16), AXES[1], swap).astype(jnp.float32)
        if shift:
            pairs = [(i, (i - shift) % sizes[0]) for i in range(sizes[0])]
            block = lax.ppermute(block.astype(jnp.bfloat16), AXES[0], pairs).astype(jnp.float32)
        total = block if total is None else total + block
    return total.astype(jnp.bfloat16)


def factor_expert(mesh):
    row = mesh.devices[0]
    try:
        cores = len({d.core_on_chip for d in row})
        xs = len({d.coords[0] for d in row})
        zs = len({d.coords[2] for d in row})
    except AttributeError:
        return None
    if cores * xs * zs != row.shape[0]:
        return None
    return zs, xs, cores


def solution(mesh):
    placed = (
        P(("groups", "expert"), None),
        P(("groups", "expert"), None),
        P(("groups", "expert"), None),
        P(),
        P("expert", None, None),
        P("expert", None, None),
    )
    factors = factor_expert(mesh)
    if factors is None or mesh.shape["expert"] > 16:
        return jax.shard_map(
            shards, mesh=mesh, in_specs=placed, out_specs=P(("groups", "expert"), None), check_vma=False
        )
    sub = Mesh(mesh.devices.reshape((mesh.shape["groups"],) + factors), ("groups",) + AXES)
    rows = P(("groups",) + AXES, None)
    placed = (rows, rows, rows, P(), P(AXES, None, None), P(AXES, None, None))
    return jax.shard_map(dense_shards, mesh=sub, in_specs=placed, out_specs=rows, check_vma=False)
```

```python
import jax
import jax.numpy as jnp
import numpy as np
from jax import lax
from jax.sharding import Mesh, PartitionSpec as P


def expert_block(rows_in, gate_up, down_proj, hidden_width):
    pair = jnp.dot(rows_in, gate_up, preferred_element_type=jnp.float32)
    active = (jax.nn.silu(pair[:, :hidden_width]) * pair[:, hidden_width:]).astype(jnp.bfloat16)
    return jnp.dot(active, down_proj, preferred_element_type=jnp.float32).astype(jnp.bfloat16)


def shards(tokens, expert_ids, gate_scores, host_expert, w_in, w_down):
    tok_rows, width_model = tokens.shape
    top_count = expert_ids.shape[1]
    hosts = lax.axis_size("expert")
    experts = host_expert.shape[0]
    capacity = 3 * tok_rows * top_count // (2 * experts)
    hidden_width = w_down.shape[1]
    routed = tok_rows * top_count
    slots = hosts * capacity
    gate_up = w_in[0]
    down_proj = w_down[0]
    expert_range = jnp.arange(experts, dtype=jnp.int32)
    host_range = jnp.arange(hosts, dtype=jnp.int32)
    placed = (host_expert[:, None] == expert_range[None, :]).astype(jnp.int32)
    host_of = jnp.sum(placed * host_range[:, None], axis=0)
    flat_ids = expert_ids.reshape(-1)
    id_match = flat_ids[:, None] == expert_range[None, :]
    dest_host = jnp.sum(jnp.where(id_match, host_of[None, :], 0), axis=1)
    row_token = jnp.arange(routed, dtype=jnp.int32) // top_count
    padded_tokens = jnp.concatenate([tokens, jnp.zeros((1, width_model), tokens.dtype)], axis=0)
    earlier = (
        lax.broadcasted_iota(jnp.int32, (routed, routed), 0)
        > lax.broadcasted_iota(jnp.int32, (routed, routed), 1)
    ).astype(jnp.bfloat16)
    dest_match = dest_host[:, None] == host_range[None, :]
    before = jnp.dot(earlier, dest_match.astype(jnp.bfloat16), preferred_element_type=jnp.float32)
    position = jnp.sum(jnp.where(dest_match, before, 0.0), axis=1).astype(jnp.int32)
    slot_of_row = dest_host * capacity + position
    source_row = jnp.full((slots + 1,), tok_rows, jnp.int32).at[slot_of_row].set(row_token)[:slots]
    outgoing = padded_tokens[source_row].reshape(hosts, capacity, width_model)
    received = lax.all_to_all(outgoing, "expert", split_axis=0, concat_axis=0, tiled=True)
    flat_in = received.reshape(-1, width_model)
    served = expert_block(flat_in, gate_up, down_proj, hidden_width).reshape(received.shape)
    returned = lax.all_to_all(served, "expert", split_axis=0, concat_axis=0, tiled=True)
    expert_rows = returned.reshape(slots, width_model)[slot_of_row]
    weights = gate_scores / jnp.sum(gate_scores, axis=1, keepdims=True)
    mixed = jnp.sum(
        weights[:, :, None]
        * expert_rows.reshape(tok_rows, top_count, width_model).astype(jnp.float32),
        axis=1,
    )
    return mixed.astype(jnp.bfloat16)


AXES = ("ez", "ex", "ec")


def gather_stage(block, axis, size):
    got = [block]
    for shift in range(1, size):
        pairs = [(i, (i + shift) % size) for i in range(size)]
        got.append(lax.ppermute(block, axis, pairs))
    return jnp.concatenate(got, axis=0)


def scatter_stage(part, axis, size):
    pieces = jnp.split(part, size, axis=0)
    total = pieces[0].astype(jnp.float32)
    for shift in range(1, size):
        pairs = [(i, (i - shift) % size) for i in range(size)]
        total = total + lax.ppermute(pieces[shift].astype(jnp.bfloat16), axis, pairs).astype(jnp.float32)
    return total


def dense_shards(tokens, expert_ids, gate_scores, host_expert, w_in, w_down):
    tok_rows, width_model = tokens.shape
    hidden_width = w_down.shape[1]
    experts = host_expert.shape[0]
    sizes = [lax.axis_size(a) for a in AXES]
    hosts = sizes[0] * sizes[1] * sizes[2]
    me = (lax.axis_index("ez") * sizes[1] + lax.axis_index("ex")) * sizes[2] + lax.axis_index("ec")
    weights = gate_scores / jnp.sum(gate_scores, axis=1, keepdims=True)
    chosen = expert_ids[:, :, None] == host_expert[None, None, :]
    per_host = jnp.sum(jnp.where(chosen, weights[:, :, None], 0.0), axis=1)
    hi = lax.reduce_precision(per_host, exponent_bits=8, mantissa_bits=7)
    rest = per_host - hi
    lo = lax.reduce_precision(rest, exponent_bits=8, mantissa_bits=7)
    lo2 = rest - lo
    extra = -(-3 * hosts // 128) * 128
    meta = jnp.concatenate([hi, lo, lo2, jnp.zeros((tok_rows, extra - 3 * hosts), jnp.float32)], axis=1)
    meta = meta.astype(jnp.bfloat16)
    carried = jnp.concatenate([tokens, meta], axis=1)
    pick = (jnp.arange(hosts, dtype=jnp.int32) == me).astype(jnp.float32)
    results = []
    held = None
    for rows in jnp.split(carried, STREAMS, axis=0):
        if held is not None:
            held, rows = lax.optimization_barrier((held, rows))
        for stage, (axis, size) in enumerate(zip(AXES, sizes)):
            rows = gather_stage(rows, axis, size)
            if stage == 1:
                held = rows
        tail = rows[:, width_model:width_model + 3 * hosts].astype(jnp.float32)
        gate = tail[:, :hosts] + tail[:, hosts:2 * hosts] + tail[:, 2 * hosts:]
        mine = jnp.sum(gate * pick[None, :], axis=1)
        out = expert_block(rows[:, :width_model], w_in[0], w_down[0], hidden_width)
        part = out.astype(jnp.float32) * mine[:, None]
        for axis, size in list(zip(AXES, sizes))[::-1]:
            part = scatter_stage(part, axis, size)
        results.append(part)
    return jnp.concatenate(results, axis=0).astype(jnp.bfloat16)


STREAMS = 2


def factor_expert(mesh):
    row = mesh.devices[0]
    try:
        cores = len({d.core_on_chip for d in row})
        xs = len({d.coords[0] for d in row})
        zs = len({d.coords[2] for d in row})
    except AttributeError:
        return None
    if cores * xs * zs != row.shape[0]:
        return None
    return zs, xs, cores


def solution(mesh):
    placed = (
        P(("groups", "expert"), None),
        P(("groups", "expert"), None),
        P(("groups", "expert"), None),
        P(),
        P("expert", None, None),
        P("expert", None, None),
    )
    factors = factor_expert(mesh)
    if factors is None or mesh.shape["expert"] > 16:
        return jax.shard_map(
            shards, mesh=mesh, in_specs=placed, out_specs=P(("groups", "expert"), None), check_vma=False
        )
    sub = Mesh(mesh.devices.reshape((mesh.shape["groups"],) + factors), ("groups",) + AXES)
    rows = P(("groups",) + AXES, None)
    placed = (rows, rows, rows, P(), P(AXES, None, None), P(AXES, None, None))
    return jax.shard_map(dense_shards, mesh=sub, in_specs=placed, out_specs=rows, check_vma=False)
```

```python
import jax
import jax.numpy as jnp
import numpy as np
from jax import lax
from jax.sharding import Mesh, PartitionSpec as P


def expert_block(rows_in, gate_up, down_proj, hidden_width):
    pair = jnp.dot(rows_in, gate_up, preferred_element_type=jnp.float32)
    active = (jax.nn.silu(pair[:, :hidden_width]) * pair[:, hidden_width:]).astype(jnp.bfloat16)
    return jnp.dot(active, down_proj, preferred_element_type=jnp.float32).astype(jnp.bfloat16)


def shards(tokens, expert_ids, gate_scores, host_expert, w_in, w_down):
    tok_rows, width_model = tokens.shape
    top_count = expert_ids.shape[1]
    hosts = lax.axis_size("expert")
    experts = host_expert.shape[0]
    capacity = 3 * tok_rows * top_count // (2 * experts)
    hidden_width = w_down.shape[1]
    routed = tok_rows * top_count
    slots = hosts * capacity
    gate_up = w_in[0]
    down_proj = w_down[0]
    expert_range = jnp.arange(experts, dtype=jnp.int32)
    host_range = jnp.arange(hosts, dtype=jnp.int32)
    placed = (host_expert[:, None] == expert_range[None, :]).astype(jnp.int32)
    host_of = jnp.sum(placed * host_range[:, None], axis=0)
    flat_ids = expert_ids.reshape(-1)
    id_match = flat_ids[:, None] == expert_range[None, :]
    dest_host = jnp.sum(jnp.where(id_match, host_of[None, :], 0), axis=1)
    row_token = jnp.arange(routed, dtype=jnp.int32) // top_count
    padded_tokens = jnp.concatenate([tokens, jnp.zeros((1, width_model), tokens.dtype)], axis=0)
    earlier = (
        lax.broadcasted_iota(jnp.int32, (routed, routed), 0)
        > lax.broadcasted_iota(jnp.int32, (routed, routed), 1)
    ).astype(jnp.bfloat16)
    dest_match = dest_host[:, None] == host_range[None, :]
    before = jnp.dot(earlier, dest_match.astype(jnp.bfloat16), preferred_element_type=jnp.float32)
    position = jnp.sum(jnp.where(dest_match, before, 0.0), axis=1).astype(jnp.int32)
    slot_of_row = dest_host * capacity + position
    source_row = jnp.full((slots + 1,), tok_rows, jnp.int32).at[slot_of_row].set(row_token)[:slots]
    outgoing = padded_tokens[source_row].reshape(hosts, capacity, width_model)
    received = lax.all_to_all(outgoing, "expert", split_axis=0, concat_axis=0, tiled=True)
    flat_in = received.reshape(-1, width_model)
    served = expert_block(flat_in, gate_up, down_proj, hidden_width).reshape(received.shape)
    returned = lax.all_to_all(served, "expert", split_axis=0, concat_axis=0, tiled=True)
    expert_rows = returned.reshape(slots, width_model)[slot_of_row]
    weights = gate_scores / jnp.sum(gate_scores, axis=1, keepdims=True)
    mixed = jnp.sum(
        weights[:, :, None]
        * expert_rows.reshape(tok_rows, top_count, width_model).astype(jnp.float32),
        axis=1,
    )
    return mixed.astype(jnp.bfloat16)


AXES = ("ez", "ex", "ec")


def gather_stage(block, axis, size):
    got = [block]
    for shift in range(1, size):
        pairs = [(i, (i + shift) % size) for i in range(size)]
        got.append(lax.ppermute(block, axis, pairs))
    return jnp.concatenate(got, axis=0)


def scatter_stage(part, axis, size):
    pieces = jnp.split(part, size, axis=0)
    total = pieces[0].astype(jnp.float32)
    for shift in range(1, size):
        pairs = [(i, (i - shift) % size) for i in range(size)]
        total = total + lax.ppermute(pieces[shift].astype(jnp.bfloat16), axis, pairs).astype(jnp.float32)
    return total


def dense_shards(tokens, expert_ids, gate_scores, host_expert, w_in, w_down):
    tok_rows, width_model = tokens.shape
    hidden_width = w_down.shape[1]
    experts = host_expert.shape[0]
    sizes = [lax.axis_size(a) for a in AXES]
    hosts = sizes[0] * sizes[1] * sizes[2]
    me = (lax.axis_index("ez") * sizes[1] + lax.axis_index("ex")) * sizes[2] + lax.axis_index("ec")
    weights = gate_scores / jnp.sum(gate_scores, axis=1, keepdims=True)
    chosen = expert_ids[:, :, None] == host_expert[None, None, :]
    per_host = jnp.sum(jnp.where(chosen, weights[:, :, None], 0.0), axis=1)
    hi = lax.reduce_precision(per_host, exponent_bits=8, mantissa_bits=7)
    rest = per_host - hi
    lo = lax.reduce_precision(rest, exponent_bits=8, mantissa_bits=7)
    lo2 = rest - lo
    extra = -(-3 * hosts // 128) * 128
    meta = jnp.concatenate([hi, lo, lo2, jnp.zeros((tok_rows, extra - 3 * hosts), jnp.float32)], axis=1)
    meta = meta.astype(jnp.bfloat16)
    carried = jnp.concatenate([tokens, meta], axis=1)
    pick = (jnp.arange(hosts, dtype=jnp.int32) == me).astype(jnp.float32)
    results = []
    for number, rows in enumerate(jnp.split(carried, STREAMS, axis=0)):
        order = list(zip(AXES, sizes))
        if number % 2:
            order = [order[1], order[0]] + order[2:]
        for axis, size in order:
            rows = gather_stage(rows, axis, size)
        tail = rows[:, width_model:width_model + 3 * hosts].astype(jnp.float32)
        gate = tail[:, :hosts] + tail[:, hosts:2 * hosts] + tail[:, 2 * hosts:]
        mine = jnp.sum(gate * pick[None, :], axis=1)
        out = expert_block(rows[:, :width_model], w_in[0], w_down[0], hidden_width)
        part = out.astype(jnp.float32) * mine[:, None]
        for axis, size in order[::-1]:
            part = scatter_stage(part, axis, size)
        results.append(part)
    return jnp.concatenate(results, axis=0).astype(jnp.bfloat16)


STREAMS = 2


def factor_expert(mesh):
    row = mesh.devices[0]
    try:
        cores = len({d.core_on_chip for d in row})
        xs = len({d.coords[0] for d in row})
        zs = len({d.coords[2] for d in row})
    except AttributeError:
        return None
    if cores * xs * zs != row.shape[0]:
        return None
    return zs, xs, cores


def solution(mesh):
    placed = (
        P(("groups", "expert"), None),
        P(("groups", "expert"), None),
        P(("groups", "expert"), None),
        P(),
        P("expert", None, None),
        P("expert", None, None),
    )
    factors = factor_expert(mesh)
    if factors is None or mesh.shape["expert"] > 16:
        return jax.shard_map(
            shards, mesh=mesh, in_specs=placed, out_specs=P(("groups", "expert"), None), check_vma=False
        )
    sub = Mesh(mesh.devices.reshape((mesh.shape["groups"],) + factors), ("groups",) + AXES)
    rows = P(("groups",) + AXES, None)
    placed = (rows, rows, rows, P(), P(AXES, None, None), P(AXES, None, None))
    return jax.shard_map(dense_shards, mesh=sub, in_specs=placed, out_specs=rows, check_vma=False)
```

```python
import jax
import jax.numpy as jnp
import numpy as np
from jax import lax
from jax.sharding import Mesh, PartitionSpec as P


def expert_block(rows_in, gate_up, down_proj, hidden_width):
    pair = jnp.dot(rows_in, gate_up, preferred_element_type=jnp.float32)
    active = (jax.nn.silu(pair[:, :hidden_width]) * pair[:, hidden_width:]).astype(jnp.bfloat16)
    return jnp.dot(active, down_proj, preferred_element_type=jnp.float32).astype(jnp.bfloat16)


def shards(tokens, expert_ids, gate_scores, host_expert, w_in, w_down):
    tok_rows, width_model = tokens.shape
    top_count = expert_ids.shape[1]
    hosts = lax.axis_size("expert")
    experts = host_expert.shape[0]
    capacity = 3 * tok_rows * top_count // (2 * experts)
    hidden_width = w_down.shape[1]
    routed = tok_rows * top_count
    slots = hosts * capacity
    gate_up = w_in[0]
    down_proj = w_down[0]
    expert_range = jnp.arange(experts, dtype=jnp.int32)
    host_range = jnp.arange(hosts, dtype=jnp.int32)
    placed = (host_expert[:, None] == expert_range[None, :]).astype(jnp.int32)
    host_of = jnp.sum(placed * host_range[:, None], axis=0)
    flat_ids = expert_ids.reshape(-1)
    id_match = flat_ids[:, None] == expert_range[None, :]
    dest_host = jnp.sum(jnp.where(id_match, host_of[None, :], 0), axis=1)
    row_token = jnp.arange(routed, dtype=jnp.int32) // top_count
    padded_tokens = jnp.concatenate([tokens, jnp.zeros((1, width_model), tokens.dtype)], axis=0)
    earlier = (
        lax.broadcasted_iota(jnp.int32, (routed, routed), 0)
        > lax.broadcasted_iota(jnp.int32, (routed, routed), 1)
    ).astype(jnp.bfloat16)
    dest_match = dest_host[:, None] == host_range[None, :]
    before = jnp.dot(earlier, dest_match.astype(jnp.bfloat16), preferred_element_type=jnp.float32)
    position = jnp.sum(jnp.where(dest_match, before, 0.0), axis=1).astype(jnp.int32)
    slot_of_row = dest_host * capacity + position
    source_row = jnp.full((slots + 1,), tok_rows, jnp.int32).at[slot_of_row].set(row_token)[:slots]
    outgoing = padded_tokens[source_row].reshape(hosts, capacity, width_model)
    received = lax.all_to_all(outgoing, "expert", split_axis=0, concat_axis=0, tiled=True)
    flat_in = received.reshape(-1, width_model)
    served = expert_block(flat_in, gate_up, down_proj, hidden_width).reshape(received.shape)
    returned = lax.all_to_all(served, "expert", split_axis=0, concat_axis=0, tiled=True)
    expert_rows = returned.reshape(slots, width_model)[slot_of_row]
    weights = gate_scores / jnp.sum(gate_scores, axis=1, keepdims=True)
    mixed = jnp.sum(
        weights[:, :, None]
        * expert_rows.reshape(tok_rows, top_count, width_model).astype(jnp.float32),
        axis=1,
    )
    return mixed.astype(jnp.bfloat16)


AXES = ("ez", "ex", "ec")


def gather_stage(block, axis, size):
    got = [block]
    for shift in range(1, size):
        pairs = [(i, (i + shift) % size) for i in range(size)]
        got.append(lax.ppermute(block, axis, pairs))
    return jnp.concatenate(got, axis=0)


def scatter_stage(part, axis, size):
    pieces = jnp.split(part, size, axis=0)
    total = pieces[0].astype(jnp.float32)
    for shift in range(1, size):
        pairs = [(i, (i - shift) % size) for i in range(size)]
        total = total + lax.ppermute(pieces[shift].astype(jnp.bfloat16), axis, pairs).astype(jnp.float32)
    return total


def dense_shards(tokens, expert_ids, gate_scores, host_expert, w_in, w_down):
    tok_rows, width_model = tokens.shape
    hidden_width = w_down.shape[1]
    experts = host_expert.shape[0]
    sizes = [lax.axis_size(a) for a in AXES]
    hosts = sizes[0] * sizes[1] * sizes[2]
    me = (lax.axis_index("ez") * sizes[1] + lax.axis_index("ex")) * sizes[2] + lax.axis_index("ec")
    weights = gate_scores / jnp.sum(gate_scores, axis=1, keepdims=True)
    chosen = expert_ids[:, :, None] == host_expert[None, None, :]
    per_host = jnp.sum(jnp.where(chosen, weights[:, :, None], 0.0), axis=1)
    hi = lax.reduce_precision(per_host, exponent_bits=8, mantissa_bits=7)
    rest = per_host - hi
    lo = lax.reduce_precision(rest, exponent_bits=8, mantissa_bits=7)
    lo2 = rest - lo
    extra = -(-3 * hosts // 128) * 128
    meta = jnp.concatenate([hi, lo, lo2, jnp.zeros((tok_rows, extra - 3 * hosts), jnp.float32)], axis=1)
    meta = meta.astype(jnp.bfloat16)
    carried = jnp.concatenate([tokens, meta], axis=1)
    pick = (jnp.arange(hosts, dtype=jnp.int32) == me).astype(jnp.float32)
    results = []
    for number, rows in enumerate(jnp.split(carried, STREAMS, axis=0)):
        order = list(zip(AXES, sizes))
        if number % 2:
            order = [order[1], order[0]] + order[2:]
        for axis, size in order:
            rows = gather_stage(rows, axis, size)
        tail = rows[:, width_model:width_model + 3 * hosts].astype(jnp.float32)
        gate = tail[:, :hosts] + tail[:, hosts:2 * hosts] + tail[:, 2 * hosts:]
        mine = jnp.sum(gate * pick[None, :], axis=1)
        out = expert_block(rows[:, :width_model], w_in[0], w_down[0], hidden_width)
        part = out.astype(jnp.float32) * mine[:, None]
        if number % 2:
            part = scatter_stage(part, AXES[2], sizes[2])
            split = part.reshape((sizes[0], sizes[1], -1) + part.shape[1:])
            total = split[:, 0]
            swap = [(i, (i + 1) % sizes[1]) for i in range(sizes[1])]
            total = total + lax.ppermute(split[:, 1].astype(jnp.bfloat16), AXES[1], swap).astype(jnp.float32)
            part = scatter_stage(total.reshape((-1,) + part.shape[1:]), AXES[0], sizes[0])
        else:
            for axis, size in order[::-1]:
                part = scatter_stage(part, axis, size)
        results.append(part)
    return jnp.concatenate(results, axis=0).astype(jnp.bfloat16)


STREAMS = 2


def factor_expert(mesh):
    row = mesh.devices[0]
    try:
        cores = len({d.core_on_chip for d in row})
        xs = len({d.coords[0] for d in row})
        zs = len({d.coords[2] for d in row})
    except AttributeError:
        return None
    if cores * xs * zs != row.shape[0]:
        return None
    return zs, xs, cores


def solution(mesh):
    placed = (
        P(("groups", "expert"), None),
        P(("groups", "expert"), None),
        P(("groups", "expert"), None),
        P(),
        P("expert", None, None),
        P("expert", None, None),
    )
    factors = factor_expert(mesh)
    if factors is None or mesh.shape["expert"] > 16:
        return jax.shard_map(
            shards, mesh=mesh, in_specs=placed, out_specs=P(("groups", "expert"), None), check_vma=False
        )
    sub = Mesh(mesh.devices.reshape((mesh.shape["groups"],) + factors), ("groups",) + AXES)
    rows = P(("groups",) + AXES, None)
    placed = (rows, rows, rows, P(), P(AXES, None, None), P(AXES, None, None))
    return jax.shard_map(dense_shards, mesh=sub, in_specs=placed, out_specs=rows, check_vma=False)
```

```python
import jax
import jax.numpy as jnp
import numpy as np
from jax import lax
from jax.sharding import Mesh, PartitionSpec as P


def expert_block(rows_in, gate_up, down_proj, hidden_width):
    pair = jnp.dot(rows_in, gate_up, preferred_element_type=jnp.float32)
    active = (jax.nn.silu(pair[:, :hidden_width]) * pair[:, hidden_width:]).astype(jnp.bfloat16)
    return jnp.dot(active, down_proj, preferred_element_type=jnp.float32).astype(jnp.bfloat16)


def shards(tokens, expert_ids, gate_scores, host_expert, w_in, w_down):
    tok_rows, width_model = tokens.shape
    top_count = expert_ids.shape[1]
    hosts = lax.axis_size("expert")
    experts = host_expert.shape[0]
    capacity = 3 * tok_rows * top_count // (2 * experts)
    hidden_width = w_down.shape[1]
    routed = tok_rows * top_count
    slots = hosts * capacity
    gate_up = w_in[0]
    down_proj = w_down[0]
    expert_range = jnp.arange(experts, dtype=jnp.int32)
    host_range = jnp.arange(hosts, dtype=jnp.int32)
    placed = (host_expert[:, None] == expert_range[None, :]).astype(jnp.int32)
    host_of = jnp.sum(placed * host_range[:, None], axis=0)
    flat_ids = expert_ids.reshape(-1)
    id_match = flat_ids[:, None] == expert_range[None, :]
    dest_host = jnp.sum(jnp.where(id_match, host_of[None, :], 0), axis=1)
    row_token = jnp.arange(routed, dtype=jnp.int32) // top_count
    padded_tokens = jnp.concatenate([tokens, jnp.zeros((1, width_model), tokens.dtype)], axis=0)
    earlier = (
        lax.broadcasted_iota(jnp.int32, (routed, routed), 0)
        > lax.broadcasted_iota(jnp.int32, (routed, routed), 1)
    ).astype(jnp.bfloat16)
    dest_match = dest_host[:, None] == host_range[None, :]
    before = jnp.dot(earlier, dest_match.astype(jnp.bfloat16), preferred_element_type=jnp.float32)
    position = jnp.sum(jnp.where(dest_match, before, 0.0), axis=1).astype(jnp.int32)
    slot_of_row = dest_host * capacity + position
    source_row = jnp.full((slots + 1,), tok_rows, jnp.int32).at[slot_of_row].set(row_token)[:slots]
    outgoing = padded_tokens[source_row].reshape(hosts, capacity, width_model)
    received = lax.all_to_all(outgoing, "expert", split_axis=0, concat_axis=0, tiled=True)
    flat_in = received.reshape(-1, width_model)
    served = expert_block(flat_in, gate_up, down_proj, hidden_width).reshape(received.shape)
    returned = lax.all_to_all(served, "expert", split_axis=0, concat_axis=0, tiled=True)
    expert_rows = returned.reshape(slots, width_model)[slot_of_row]
    weights = gate_scores / jnp.sum(gate_scores, axis=1, keepdims=True)
    mixed = jnp.sum(
        weights[:, :, None]
        * expert_rows.reshape(tok_rows, top_count, width_model).astype(jnp.float32),
        axis=1,
    )
    return mixed.astype(jnp.bfloat16)


AXES = ("ez", "ex", "ec")


def gather_stage(block, axis, size):
    got = [block]
    for shift in range(1, size):
        pairs = [(i, (i + shift) % size) for i in range(size)]
        got.append(lax.ppermute(block, axis, pairs))
    return jnp.concatenate(got, axis=0)


def scatter_stage(part, axis, size):
    pieces = jnp.split(part, size, axis=0)
    total = pieces[0].astype(jnp.float32)
    for shift in range(1, size):
        pairs = [(i, (i - shift) % size) for i in range(size)]
        total = total + lax.ppermute(pieces[shift].astype(jnp.bfloat16), axis, pairs).astype(jnp.float32)
    return total


def dense_shards(tokens, expert_ids, gate_scores, host_expert, w_in, w_down):
    tok_rows, width_model = tokens.shape
    hidden_width = w_down.shape[1]
    experts = host_expert.shape[0]
    sizes = [lax.axis_size(a) for a in AXES]
    hosts = sizes[0] * sizes[1] * sizes[2]
    me = (lax.axis_index("ez") * sizes[1] + lax.axis_index("ex")) * sizes[2] + lax.axis_index("ec")
    weights = gate_scores / jnp.sum(gate_scores, axis=1, keepdims=True)
    chosen = expert_ids[:, :, None] == host_expert[None, None, :]
    per_host = jnp.sum(jnp.where(chosen, weights[:, :, None], 0.0), axis=1)
    hi = lax.reduce_precision(per_host, exponent_bits=8, mantissa_bits=7)
    rest = per_host - hi
    lo = lax.reduce_precision(rest, exponent_bits=8, mantissa_bits=7)
    lo2 = rest - lo
    extra = -(-3 * hosts // 128) * 128
    meta = jnp.concatenate([hi, lo, lo2, jnp.zeros((tok_rows, extra - 3 * hosts), jnp.float32)], axis=1)
    meta = meta.astype(jnp.bfloat16)
    carried = jnp.concatenate([tokens, meta], axis=1)
    pick = (jnp.arange(hosts, dtype=jnp.int32) == me).astype(jnp.float32)
    results = []
    for number, rows in enumerate(jnp.split(carried, STREAMS, axis=0)):
        order = list(zip(AXES, sizes))
        if number % 2:
            order = [order[1], order[0]] + order[2:]
        for axis, size in order:
            rows = gather_stage(rows, axis, size)
        tail = rows[:, width_model:width_model + 3 * hosts].astype(jnp.float32)
        gate = tail[:, :hosts] + tail[:, hosts:2 * hosts] + tail[:, 2 * hosts:]
        mine = jnp.sum(gate * pick[None, :], axis=1)
        out = expert_block(rows[:, :width_model], w_in[0], w_down[0], hidden_width)
        part = out.astype(jnp.float32) * mine[:, None]
        if number % 2:
            part = scatter_stage(part, AXES[2], sizes[2])
            _, part = lax.optimization_barrier((x_back, part))
            split = part.reshape((sizes[0], sizes[1], -1) + part.shape[1:])
            total = split[:, 0]
            swap = [(i, (i + 1) % sizes[1]) for i in range(sizes[1])]
            total = total + lax.ppermute(split[:, 1].astype(jnp.bfloat16), AXES[1], swap).astype(jnp.float32)
            part = scatter_stage(total.reshape((-1,) + part.shape[1:]), AXES[0], sizes[0])
        else:
            for axis, size in order[::-1]:
                part = scatter_stage(part, axis, size)
                if axis == AXES[1]:
                    x_back = part
        results.append(part)
    return jnp.concatenate(results, axis=0).astype(jnp.bfloat16)


STREAMS = 2


def factor_expert(mesh):
    row = mesh.devices[0]
    try:
        cores = len({d.core_on_chip for d in row})
        xs = len({d.coords[0] for d in row})
        zs = len({d.coords[2] for d in row})
    except AttributeError:
        return None
    if cores * xs * zs != row.shape[0]:
        return None
    return zs, xs, cores


def solution(mesh):
    placed = (
        P(("groups", "expert"), None),
        P(("groups", "expert"), None),
        P(("groups", "expert"), None),
        P(),
        P("expert", None, None),
        P("expert", None, None),
    )
    factors = factor_expert(mesh)
    if factors is None or mesh.shape["expert"] > 16:
        return jax.shard_map(
            shards, mesh=mesh, in_specs=placed, out_specs=P(("groups", "expert"), None), check_vma=False
        )
    sub = Mesh(mesh.devices.reshape((mesh.shape["groups"],) + factors), ("groups",) + AXES)
    rows = P(("groups",) + AXES, None)
    placed = (rows, rows, rows, P(), P(AXES, None, None), P(AXES, None, None))
    return jax.shard_map(dense_shards, mesh=sub, in_specs=placed, out_specs=rows, check_vma=False)
```

```python
import jax
import jax.numpy as jnp
import numpy as np
from jax import lax
from jax.sharding import Mesh, PartitionSpec as P


def expert_block(rows_in, gate_up, down_proj, hidden_width):
    pair = jnp.dot(rows_in, gate_up, preferred_element_type=jnp.float32)
    active = (jax.nn.silu(pair[:, :hidden_width]) * pair[:, hidden_width:]).astype(jnp.bfloat16)
    return jnp.dot(active, down_proj, preferred_element_type=jnp.float32).astype(jnp.bfloat16)


def shards(tokens, expert_ids, gate_scores, host_expert, w_in, w_down):
    tok_rows, width_model = tokens.shape
    top_count = expert_ids.shape[1]
    hosts = lax.axis_size("expert")
    experts = host_expert.shape[0]
    capacity = 3 * tok_rows * top_count // (2 * experts)
    hidden_width = w_down.shape[1]
    routed = tok_rows * top_count
    slots = hosts * capacity
    gate_up = w_in[0]
    down_proj = w_down[0]
    expert_range = jnp.arange(experts, dtype=jnp.int32)
    host_range = jnp.arange(hosts, dtype=jnp.int32)
    placed = (host_expert[:, None] == expert_range[None, :]).astype(jnp.int32)
    host_of = jnp.sum(placed * host_range[:, None], axis=0)
    flat_ids = expert_ids.reshape(-1)
    id_match = flat_ids[:, None] == expert_range[None, :]
    dest_host = jnp.sum(jnp.where(id_match, host_of[None, :], 0), axis=1)
    row_token = jnp.arange(routed, dtype=jnp.int32) // top_count
    padded_tokens = jnp.concatenate([tokens, jnp.zeros((1, width_model), tokens.dtype)], axis=0)
    earlier = (
        lax.broadcasted_iota(jnp.int32, (routed, routed), 0)
        > lax.broadcasted_iota(jnp.int32, (routed, routed), 1)
    ).astype(jnp.bfloat16)
    dest_match = dest_host[:, None] == host_range[None, :]
    before = jnp.dot(earlier, dest_match.astype(jnp.bfloat16), preferred_element_type=jnp.float32)
    position = jnp.sum(jnp.where(dest_match, before, 0.0), axis=1).astype(jnp.int32)
    slot_of_row = dest_host * capacity + position
    source_row = jnp.full((slots + 1,), tok_rows, jnp.int32).at[slot_of_row].set(row_token)[:slots]
    outgoing = padded_tokens[source_row].reshape(hosts, capacity, width_model)
    received = lax.all_to_all(outgoing, "expert", split_axis=0, concat_axis=0, tiled=True)
    flat_in = received.reshape(-1, width_model)
    served = expert_block(flat_in, gate_up, down_proj, hidden_width).reshape(received.shape)
    returned = lax.all_to_all(served, "expert", split_axis=0, concat_axis=0, tiled=True)
    expert_rows = returned.reshape(slots, width_model)[slot_of_row]
    weights = gate_scores / jnp.sum(gate_scores, axis=1, keepdims=True)
    mixed = jnp.sum(
        weights[:, :, None]
        * expert_rows.reshape(tok_rows, top_count, width_model).astype(jnp.float32),
        axis=1,
    )
    return mixed.astype(jnp.bfloat16)


AXES = ("ez", "ex", "ec")


def gather_stage(block, axis, size):
    got = [block]
    for shift in range(1, size):
        pairs = [(i, (i + shift) % size) for i in range(size)]
        got.append(lax.ppermute(block, axis, pairs))
    return jnp.concatenate(got, axis=0)


def scatter_stage(part, axis, size):
    pieces = jnp.split(part, size, axis=0)
    total = pieces[0].astype(jnp.float32)
    for shift in range(1, size):
        pairs = [(i, (i - shift) % size) for i in range(size)]
        total = total + lax.ppermute(pieces[shift].astype(jnp.bfloat16), axis, pairs).astype(jnp.float32)
    return total


def dense_shards(tokens, expert_ids, gate_scores, host_expert, w_in, w_down):
    tok_rows, width_model = tokens.shape
    hidden_width = w_down.shape[1]
    experts = host_expert.shape[0]
    sizes = [lax.axis_size(a) for a in AXES]
    hosts = sizes[0] * sizes[1] * sizes[2]
    me = (lax.axis_index("ez") * sizes[1] + lax.axis_index("ex")) * sizes[2] + lax.axis_index("ec")
    weights = gate_scores / jnp.sum(gate_scores, axis=1, keepdims=True)
    chosen = expert_ids[:, :, None] == host_expert[None, None, :]
    per_host = jnp.sum(jnp.where(chosen, weights[:, :, None], 0.0), axis=1)
    hi = lax.reduce_precision(per_host, exponent_bits=8, mantissa_bits=7)
    rest = per_host - hi
    lo = lax.reduce_precision(rest, exponent_bits=8, mantissa_bits=7)
    lo2 = rest - lo
    extra = -(-3 * hosts // 128) * 128
    meta = jnp.concatenate([hi, lo, lo2, jnp.zeros((tok_rows, extra - 3 * hosts), jnp.float32)], axis=1)
    meta = meta.astype(jnp.bfloat16)
    carried = jnp.concatenate([tokens, meta], axis=1)
    pick = (jnp.arange(hosts, dtype=jnp.int32) == me).astype(jnp.float32)
    partner = me + 1 - 2 * lax.axis_index(AXES[2])
    pick_other = (jnp.arange(hosts, dtype=jnp.int32) == partner).astype(jnp.float32)
    results = []
    held = None
    for rows in jnp.split(carried, STREAMS, axis=0):
        if held is not None:
            held, rows = lax.optimization_barrier((held, rows))
        rows = gather_stage(rows, AXES[0], sizes[0])
        held = rows
        for axis, size in zip(AXES[1:], sizes[1:]):
            rows = gather_stage(rows, axis, size)
        tail = rows[:, width_model:width_model + 3 * hosts].astype(jnp.float32)
        gate = tail[:, :hosts] + tail[:, hosts:2 * hosts] + tail[:, 2 * hosts:]
        mine = jnp.sum(gate * pick[None, :], axis=1)
        out = expert_block(rows[:, :width_model], w_in[0], w_down[0], hidden_width)
        theirs = jnp.sum(gate * pick_other[None, :], axis=1)
        kept, sent = jnp.split(out, 2, axis=0)
        pairs = [(i, (i + 1) % sizes[2]) for i in range(sizes[2])]
        back = lax.ppermute(sent, AXES[2], pairs).astype(jnp.float32)
        half = kept.shape[0]
        part = kept.astype(jnp.float32) * mine[:half, None] + back * theirs[:half, None]
        for axis, size in list(zip(AXES[:2], sizes[:2]))[::-1]:
            part = scatter_stage(part, axis, size)
        results.append(part)
    return jnp.concatenate(results, axis=0).astype(jnp.bfloat16)


STREAMS = 2


def factor_expert(mesh):
    row = mesh.devices[0]
    try:
        cores = len({d.core_on_chip for d in row})
        xs = len({d.coords[0] for d in row})
        zs = len({d.coords[2] for d in row})
    except AttributeError:
        return None
    if cores * xs * zs != row.shape[0]:
        return None
    return zs, xs, cores


def solution(mesh):
    placed = (
        P(("groups", "expert"), None),
        P(("groups", "expert"), None),
        P(("groups", "expert"), None),
        P(),
        P("expert", None, None),
        P("expert", None, None),
    )
    factors = factor_expert(mesh)
    if factors is None or mesh.shape["expert"] > 16:
        return jax.shard_map(
            shards, mesh=mesh, in_specs=placed, out_specs=P(("groups", "expert"), None), check_vma=False
        )
    sub = Mesh(mesh.devices.reshape((mesh.shape["groups"],) + factors), ("groups",) + AXES)
    rows = P(("groups",) + AXES, None)
    placed = (rows, rows, rows, P(), P(AXES, None, None), P(AXES, None, None))
    return jax.shard_map(dense_shards, mesh=sub, in_specs=placed, out_specs=rows, check_vma=False)
```

```python
import jax
import jax.numpy as jnp
import numpy as np
from jax import lax
from jax.sharding import Mesh, PartitionSpec as P


def expert_block(rows_in, gate_up, down_proj, hidden_width):
    pair = jnp.dot(rows_in, gate_up, preferred_element_type=jnp.float32)
    active = (jax.nn.silu(pair[:, :hidden_width]) * pair[:, hidden_width:]).astype(jnp.bfloat16)
    return jnp.dot(active, down_proj, preferred_element_type=jnp.float32).astype(jnp.bfloat16)


def shards(tokens, expert_ids, gate_scores, host_expert, w_in, w_down):
    tok_rows, width_model = tokens.shape
    top_count = expert_ids.shape[1]
    hosts = lax.axis_size("expert")
    experts = host_expert.shape[0]
    capacity = 3 * tok_rows * top_count // (2 * experts)
    hidden_width = w_down.shape[1]
    routed = tok_rows * top_count
    slots = hosts * capacity
    gate_up = w_in[0]
    down_proj = w_down[0]
    expert_range = jnp.arange(experts, dtype=jnp.int32)
    host_range = jnp.arange(hosts, dtype=jnp.int32)
    placed = (host_expert[:, None] == expert_range[None, :]).astype(jnp.int32)
    host_of = jnp.sum(placed * host_range[:, None], axis=0)
    flat_ids = expert_ids.reshape(-1)
    id_match = flat_ids[:, None] == expert_range[None, :]
    dest_host = jnp.sum(jnp.where(id_match, host_of[None, :], 0), axis=1)
    row_token = jnp.arange(routed, dtype=jnp.int32) // top_count
    padded_tokens = jnp.concatenate([tokens, jnp.zeros((1, width_model), tokens.dtype)], axis=0)
    earlier = (
        lax.broadcasted_iota(jnp.int32, (routed, routed), 0)
        > lax.broadcasted_iota(jnp.int32, (routed, routed), 1)
    ).astype(jnp.bfloat16)
    dest_match = dest_host[:, None] == host_range[None, :]
    before = jnp.dot(earlier, dest_match.astype(jnp.bfloat16), preferred_element_type=jnp.float32)
    position = jnp.sum(jnp.where(dest_match, before, 0.0), axis=1).astype(jnp.int32)
    slot_of_row = dest_host * capacity + position
    source_row = jnp.full((slots + 1,), tok_rows, jnp.int32).at[slot_of_row].set(row_token)[:slots]
    outgoing = padded_tokens[source_row].reshape(hosts, capacity, width_model)
    received = lax.all_to_all(outgoing, "expert", split_axis=0, concat_axis=0, tiled=True)
    flat_in = received.reshape(-1, width_model)
    served = expert_block(flat_in, gate_up, down_proj, hidden_width).reshape(received.shape)
    returned = lax.all_to_all(served, "expert", split_axis=0, concat_axis=0, tiled=True)
    expert_rows = returned.reshape(slots, width_model)[slot_of_row]
    weights = gate_scores / jnp.sum(gate_scores, axis=1, keepdims=True)
    mixed = jnp.sum(
        weights[:, :, None]
        * expert_rows.reshape(tok_rows, top_count, width_model).astype(jnp.float32),
        axis=1,
    )
    return mixed.astype(jnp.bfloat16)


AXES = ("ez", "ex", "ec")


def gather_stage(block, axis, size):
    got = [block]
    for shift in range(1, size):
        pairs = [(i, (i + shift) % size) for i in range(size)]
        got.append(lax.ppermute(block, axis, pairs))
    return jnp.concatenate(got, axis=0)


def scatter_stage(part, axis, size):
    pieces = jnp.split(part, size, axis=0)
    total = pieces[0].astype(jnp.float32)
    for shift in range(1, size):
        pairs = [(i, (i - shift) % size) for i in range(size)]
        total = total + lax.ppermute(pieces[shift].astype(jnp.bfloat16), axis, pairs).astype(jnp.float32)
    return total


def dense_shards(tokens, expert_ids, gate_scores, host_expert, w_in, w_down):
    tok_rows, width_model = tokens.shape
    hidden_width = w_down.shape[1]
    experts = host_expert.shape[0]
    sizes = [lax.axis_size(a) for a in AXES]
    hosts = sizes[0] * sizes[1] * sizes[2]
    me = (lax.axis_index("ez") * sizes[1] + lax.axis_index("ex")) * sizes[2] + lax.axis_index("ec")
    weights = gate_scores / jnp.sum(gate_scores, axis=1, keepdims=True)
    chosen = expert_ids[:, :, None] == host_expert[None, None, :]
    per_host = jnp.sum(jnp.where(chosen, weights[:, :, None], 0.0), axis=1)
    hi = lax.reduce_precision(per_host, exponent_bits=8, mantissa_bits=7)
    rest = per_host - hi
    lo = lax.reduce_precision(rest, exponent_bits=8, mantissa_bits=7)
    lo2 = rest - lo
    extra = -(-3 * hosts // 128) * 128
    meta = jnp.concatenate([hi, lo, lo2, jnp.zeros((tok_rows, extra - 3 * hosts), jnp.float32)], axis=1)
    meta = meta.astype(jnp.bfloat16)
    carried = jnp.concatenate([tokens, meta], axis=1)
    pick = (jnp.arange(hosts, dtype=jnp.int32) == me).astype(jnp.float32)
    results = []
    held = None
    first = tok_rows * 5 // 8 // 8 * 8
    for rows in (carried[:first], carried[first:]):
        if held is not None:
            held, rows = lax.optimization_barrier((held, rows))
        rows = gather_stage(rows, AXES[0], sizes[0])
        held = rows
        for axis, size in zip(AXES[1:], sizes[1:]):
            rows = gather_stage(rows, axis, size)
        tail = rows[:, width_model:width_model + 3 * hosts].astype(jnp.float32)
        gate = tail[:, :hosts] + tail[:, hosts:2 * hosts] + tail[:, 2 * hosts:]
        mine = jnp.sum(gate * pick[None, :], axis=1)
        out = expert_block(rows[:, :width_model], w_in[0], w_down[0], hidden_width)
        part = out.astype(jnp.float32) * mine[:, None]
        for axis, size in list(zip(AXES, sizes))[::-1]:
            part = scatter_stage(part, axis, size)
        results.append(part)
    return jnp.concatenate(results, axis=0).astype(jnp.bfloat16)


def factor_expert(mesh):
    row = mesh.devices[0]
    try:
        cores = len({d.core_on_chip for d in row})
        xs = len({d.coords[0] for d in row})
        zs = len({d.coords[2] for d in row})
    except AttributeError:
        return None
    if cores * xs * zs != row.shape[0]:
        return None
    return zs, xs, cores


def solution(mesh):
    placed = (
        P(("groups", "expert"), None),
        P(("groups", "expert"), None),
        P(("groups", "expert"), None),
        P(),
        P("expert", None, None),
        P("expert", None, None),
    )
    factors = factor_expert(mesh)
    if factors is None or mesh.shape["expert"] > 16:
        return jax.shard_map(
            shards, mesh=mesh, in_specs=placed, out_specs=P(("groups", "expert"), None), check_vma=False
        )
    sub = Mesh(mesh.devices.reshape((mesh.shape["groups"],) + factors), ("groups",) + AXES)
    rows = P(("groups",) + AXES, None)
    placed = (rows, rows, rows, P(), P(AXES, None, None), P(AXES, None, None))
    return jax.shard_map(dense_shards, mesh=sub, in_specs=placed, out_specs=rows, check_vma=False)
```

```python
import jax
import jax.numpy as jnp
import numpy as np
from jax import lax
from jax.sharding import Mesh, PartitionSpec as P


def expert_block(rows_in, gate_up, down_proj, hidden_width):
    pair = jnp.dot(rows_in, gate_up, preferred_element_type=jnp.float32)
    active = (jax.nn.silu(pair[:, :hidden_width]) * pair[:, hidden_width:]).astype(jnp.bfloat16)
    return jnp.dot(active, down_proj, preferred_element_type=jnp.float32).astype(jnp.bfloat16)


def shards(tokens, expert_ids, gate_scores, host_expert, w_in, w_down):
    tok_rows, width_model = tokens.shape
    top_count = expert_ids.shape[1]
    hosts = lax.axis_size("expert")
    experts = host_expert.shape[0]
    capacity = 3 * tok_rows * top_count // (2 * experts)
    hidden_width = w_down.shape[1]
    routed = tok_rows * top_count
    slots = hosts * capacity
    gate_up = w_in[0]
    down_proj = w_down[0]
    expert_range = jnp.arange(experts, dtype=jnp.int32)
    host_range = jnp.arange(hosts, dtype=jnp.int32)
    placed = (host_expert[:, None] == expert_range[None, :]).astype(jnp.int32)
    host_of = jnp.sum(placed * host_range[:, None], axis=0)
    flat_ids = expert_ids.reshape(-1)
    id_match = flat_ids[:, None] == expert_range[None, :]
    dest_host = jnp.sum(jnp.where(id_match, host_of[None, :], 0), axis=1)
    row_token = jnp.arange(routed, dtype=jnp.int32) // top_count
    padded_tokens = jnp.concatenate([tokens, jnp.zeros((1, width_model), tokens.dtype)], axis=0)
    earlier = (
        lax.broadcasted_iota(jnp.int32, (routed, routed), 0)
        > lax.broadcasted_iota(jnp.int32, (routed, routed), 1)
    ).astype(jnp.bfloat16)
    dest_match = dest_host[:, None] == host_range[None, :]
    before = jnp.dot(earlier, dest_match.astype(jnp.bfloat16), preferred_element_type=jnp.float32)
    position = jnp.sum(jnp.where(dest_match, before, 0.0), axis=1).astype(jnp.int32)
    slot_of_row = dest_host * capacity + position
    source_row = jnp.full((slots + 1,), tok_rows, jnp.int32).at[slot_of_row].set(row_token)[:slots]
    outgoing = padded_tokens[source_row].reshape(hosts, capacity, width_model)
    received = lax.all_to_all(outgoing, "expert", split_axis=0, concat_axis=0, tiled=True)
    flat_in = received.reshape(-1, width_model)
    served = expert_block(flat_in, gate_up, down_proj, hidden_width).reshape(received.shape)
    returned = lax.all_to_all(served, "expert", split_axis=0, concat_axis=0, tiled=True)
    expert_rows = returned.reshape(slots, width_model)[slot_of_row]
    weights = gate_scores / jnp.sum(gate_scores, axis=1, keepdims=True)
    mixed = jnp.sum(
        weights[:, :, None]
        * expert_rows.reshape(tok_rows, top_count, width_model).astype(jnp.float32),
        axis=1,
    )
    return mixed.astype(jnp.bfloat16)


AXES = ("ez", "ex", "ec")


def gather_stage(block, axis, size):
    got = [block]
    for shift in range(1, size):
        pairs = [(i, (i + shift) % size) for i in range(size)]
        got.append(lax.ppermute(block, axis, pairs))
    return jnp.concatenate(got, axis=0)


def scatter_stage(part, axis, size):
    pieces = jnp.split(part, size, axis=0)
    total = pieces[0].astype(jnp.float32)
    for shift in range(1, size):
        pairs = [(i, (i - shift) % size) for i in range(size)]
        total = total + lax.ppermute(pieces[shift].astype(jnp.bfloat16), axis, pairs).astype(jnp.float32)
    return total


def dense_shards(tokens, expert_ids, gate_scores, host_expert, w_in, w_down):
    tok_rows, width_model = tokens.shape
    hidden_width = w_down.shape[1]
    experts = host_expert.shape[0]
    sizes = [lax.axis_size(a) for a in AXES]
    hosts = sizes[0] * sizes[1] * sizes[2]
    me = (lax.axis_index("ez") * sizes[1] + lax.axis_index("ex")) * sizes[2] + lax.axis_index("ec")
    weights = gate_scores / jnp.sum(gate_scores, axis=1, keepdims=True)
    chosen = expert_ids[:, :, None] == host_expert[None, None, :]
    per_host = jnp.sum(jnp.where(chosen, weights[:, :, None], 0.0), axis=1)
    hi = lax.reduce_precision(per_host, exponent_bits=8, mantissa_bits=7)
    rest = per_host - hi
    lo = lax.reduce_precision(rest, exponent_bits=8, mantissa_bits=7)
    lo2 = rest - lo
    extra = -(-3 * hosts // 128) * 128
    meta = jnp.concatenate([hi, lo, lo2, jnp.zeros((tok_rows, extra - 3 * hosts), jnp.float32)], axis=1)
    meta = meta.astype(jnp.bfloat16)
    carried = jnp.concatenate([tokens, meta], axis=1)
    pick = (jnp.arange(hosts, dtype=jnp.int32) == me).astype(jnp.float32)
    results = []
    held = None
    first = tok_rows * 3 // 8 // 8 * 8
    for rows in (carried[:first], carried[first:]):
        if held is not None:
            held, rows = lax.optimization_barrier((held, rows))
        rows = gather_stage(rows, AXES[0], sizes[0])
        held = rows
        for axis, size in zip(AXES[1:], sizes[1:]):
            rows = gather_stage(rows, axis, size)
        tail = rows[:, width_model:width_model + 3 * hosts].astype(jnp.float32)
        gate = tail[:, :hosts] + tail[:, hosts:2 * hosts] + tail[:, 2 * hosts:]
        mine = jnp.sum(gate * pick[None, :], axis=1)
        out = expert_block(rows[:, :width_model], w_in[0], w_down[0], hidden_width)
        part = out.astype(jnp.float32) * mine[:, None]
        for axis, size in list(zip(AXES, sizes))[::-1]:
            part = scatter_stage(part, axis, size)
        results.append(part)
    return jnp.concatenate(results, axis=0).astype(jnp.bfloat16)


def factor_expert(mesh):
    row = mesh.devices[0]
    try:
        cores = len({d.core_on_chip for d in row})
        xs = len({d.coords[0] for d in row})
        zs = len({d.coords[2] for d in row})
    except AttributeError:
        return None
    if cores * xs * zs != row.shape[0]:
        return None
    return zs, xs, cores


def solution(mesh):
    placed = (
        P(("groups", "expert"), None),
        P(("groups", "expert"), None),
        P(("groups", "expert"), None),
        P(),
        P("expert", None, None),
        P("expert", None, None),
    )
    factors = factor_expert(mesh)
    if factors is None or mesh.shape["expert"] > 16:
        return jax.shard_map(
            shards, mesh=mesh, in_specs=placed, out_specs=P(("groups", "expert"), None), check_vma=False
        )
    sub = Mesh(mesh.devices.reshape((mesh.shape["groups"],) + factors), ("groups",) + AXES)
    rows = P(("groups",) + AXES, None)
    placed = (rows, rows, rows, P(), P(AXES, None, None), P(AXES, None, None))
    return jax.shard_map(dense_shards, mesh=sub, in_specs=placed, out_specs=rows, check_vma=False)
```

```python
import jax
import jax.numpy as jnp
import numpy as np
from jax import lax
from jax.sharding import Mesh, PartitionSpec as P


def expert_block(rows_in, gate_up, down_proj, hidden_width):
    pair = jnp.dot(rows_in, gate_up, preferred_element_type=jnp.float32)
    active = (jax.nn.silu(pair[:, :hidden_width]) * pair[:, hidden_width:]).astype(jnp.bfloat16)
    return jnp.dot(active, down_proj, preferred_element_type=jnp.float32).astype(jnp.bfloat16)


def shards(tokens, expert_ids, gate_scores, host_expert, w_in, w_down):
    tok_rows, width_model = tokens.shape
    top_count = expert_ids.shape[1]
    hosts = lax.axis_size("expert")
    experts = host_expert.shape[0]
    capacity = 3 * tok_rows * top_count // (2 * experts)
    hidden_width = w_down.shape[1]
    routed = tok_rows * top_count
    slots = hosts * capacity
    gate_up = w_in[0]
    down_proj = w_down[0]
    expert_range = jnp.arange(experts, dtype=jnp.int32)
    host_range = jnp.arange(hosts, dtype=jnp.int32)
    placed = (host_expert[:, None] == expert_range[None, :]).astype(jnp.int32)
    host_of = jnp.sum(placed * host_range[:, None], axis=0)
    flat_ids = expert_ids.reshape(-1)
    id_match = flat_ids[:, None] == expert_range[None, :]
    dest_host = jnp.sum(jnp.where(id_match, host_of[None, :], 0), axis=1)
    row_token = jnp.arange(routed, dtype=jnp.int32) // top_count
    padded_tokens = jnp.concatenate([tokens, jnp.zeros((1, width_model), tokens.dtype)], axis=0)
    earlier = (
        lax.broadcasted_iota(jnp.int32, (routed, routed), 0)
        > lax.broadcasted_iota(jnp.int32, (routed, routed), 1)
    ).astype(jnp.bfloat16)
    dest_match = dest_host[:, None] == host_range[None, :]
    before = jnp.dot(earlier, dest_match.astype(jnp.bfloat16), preferred_element_type=jnp.float32)
    position = jnp.sum(jnp.where(dest_match, before, 0.0), axis=1).astype(jnp.int32)
    slot_of_row = dest_host * capacity + position
    source_row = jnp.full((slots + 1,), tok_rows, jnp.int32).at[slot_of_row].set(row_token)[:slots]
    outgoing = padded_tokens[source_row].reshape(hosts, capacity, width_model)
    received = lax.all_to_all(outgoing, "expert", split_axis=0, concat_axis=0, tiled=True)
    flat_in = received.reshape(-1, width_model)
    served = expert_block(flat_in, gate_up, down_proj, hidden_width).reshape(received.shape)
    returned = lax.all_to_all(served, "expert", split_axis=0, concat_axis=0, tiled=True)
    expert_rows = returned.reshape(slots, width_model)[slot_of_row]
    weights = gate_scores / jnp.sum(gate_scores, axis=1, keepdims=True)
    mixed = jnp.sum(
        weights[:, :, None]
        * expert_rows.reshape(tok_rows, top_count, width_model).astype(jnp.float32),
        axis=1,
    )
    return mixed.astype(jnp.bfloat16)


AXES = ("ez", "ex", "ec")


def gather_stage(block, axis, size):
    got = [block]
    for shift in range(1, size):
        pairs = [(i, (i + shift) % size) for i in range(size)]
        got.append(lax.ppermute(block, axis, pairs))
    return jnp.concatenate(got, axis=0)


def scatter_stage(part, axis, size):
    pieces = jnp.split(part, size, axis=0)
    total = pieces[0].astype(jnp.float32)
    for shift in range(1, size):
        pairs = [(i, (i - shift) % size) for i in range(size)]
        total = total + lax.ppermute(pieces[shift].astype(jnp.bfloat16), axis, pairs).astype(jnp.float32)
    return total


def dense_shards(tokens, expert_ids, gate_scores, host_expert, w_in, w_down):
    tok_rows, width_model = tokens.shape
    hidden_width = w_down.shape[1]
    experts = host_expert.shape[0]
    sizes = [lax.axis_size(a) for a in AXES]
    hosts = sizes[0] * sizes[1] * sizes[2]
    me = (lax.axis_index("ez") * sizes[1] + lax.axis_index("ex")) * sizes[2] + lax.axis_index("ec")
    weights = gate_scores / jnp.sum(gate_scores, axis=1, keepdims=True)
    chosen = expert_ids[:, :, None] == host_expert[None, None, :]
    per_host = jnp.sum(jnp.where(chosen, weights[:, :, None], 0.0), axis=1)
    hi = lax.reduce_precision(per_host, exponent_bits=8, mantissa_bits=7)
    rest = per_host - hi
    lo = lax.reduce_precision(rest, exponent_bits=8, mantissa_bits=7)
    lo2 = rest - lo
    extra = -(-3 * hosts // 128) * 128
    meta = jnp.concatenate([hi, lo, lo2, jnp.zeros((tok_rows, extra - 3 * hosts), jnp.float32)], axis=1)
    meta = meta.astype(jnp.bfloat16)
    carried = jnp.concatenate([tokens, meta], axis=1)
    pick = (jnp.arange(hosts, dtype=jnp.int32) == me).astype(jnp.float32)
    results = []
    held = None
    for rows in jnp.split(carried, STREAMS, axis=0):
        if held is not None:
            held, rows = lax.optimization_barrier((held, rows))
        rows = gather_stage(rows, AXES[0], sizes[0])
        held = rows
        for axis, size in zip(AXES[1:], sizes[1:]):
            rows = gather_stage(rows, axis, size)
        tail = rows[:, width_model:width_model + 3 * hosts].astype(jnp.float32)
        gate = tail[:, :hosts] + tail[:, hosts:2 * hosts] + tail[:, 2 * hosts:]
        mine = jnp.sum(gate * pick[None, :], axis=1)
        out = expert_block(rows[:, :width_model], w_in[0], w_down[0], hidden_width)
        part = out.astype(jnp.float32) * mine[:, None]
        for axis, size in list(zip(AXES, sizes))[::-1]:
            if axis == AXES[0] and results:
                _, part = lax.optimization_barrier((results[-1], part))
            part = scatter_stage(part, axis, size)
        results.append(part)
    return jnp.concatenate(results, axis=0).astype(jnp.bfloat16)


STREAMS = 2


def factor_expert(mesh):
    row = mesh.devices[0]
    try:
        cores = len({d.core_on_chip for d in row})
        xs = len({d.coords[0] for d in row})
        zs = len({d.coords[2] for d in row})
    except AttributeError:
        return None
    if cores * xs * zs != row.shape[0]:
        return None
    return zs, xs, cores


def solution(mesh):
    placed = (
        P(("groups", "expert"), None),
        P(("groups", "expert"), None),
        P(("groups", "expert"), None),
        P(),
        P("expert", None, None),
        P("expert", None, None),
    )
    factors = factor_expert(mesh)
    if factors is None or mesh.shape["expert"] > 16:
        return jax.shard_map(
            shards, mesh=mesh, in_specs=placed, out_specs=P(("groups", "expert"), None), check_vma=False
        )
    sub = Mesh(mesh.devices.reshape((mesh.shape["groups"],) + factors), ("groups",) + AXES)
    rows = P(("groups",) + AXES, None)
    placed = (rows, rows, rows, P(), P(AXES, None, None), P(AXES, None, None))
    return jax.shard_map(dense_shards, mesh=sub, in_specs=placed, out_specs=rows, check_vma=False)
```

```python
import jax
import jax.numpy as jnp
import numpy as np
from jax import lax
from jax.sharding import Mesh, PartitionSpec as P


def expert_block(rows_in, gate_up, down_proj, hidden_width):
    pair = jnp.dot(rows_in, gate_up, preferred_element_type=jnp.float32)
    active = (jax.nn.silu(pair[:, :hidden_width]) * pair[:, hidden_width:]).astype(jnp.bfloat16)
    return jnp.dot(active, down_proj, preferred_element_type=jnp.float32).astype(jnp.bfloat16)


def shards(tokens, expert_ids, gate_scores, host_expert, w_in, w_down):
    tok_rows, width_model = tokens.shape
    top_count = expert_ids.shape[1]
    hosts = lax.axis_size("expert")
    experts = host_expert.shape[0]
    capacity = 3 * tok_rows * top_count // (2 * experts)
    hidden_width = w_down.shape[1]
    routed = tok_rows * top_count
    slots = hosts * capacity
    gate_up = w_in[0]
    down_proj = w_down[0]
    expert_range = jnp.arange(experts, dtype=jnp.int32)
    host_range = jnp.arange(hosts, dtype=jnp.int32)
    placed = (host_expert[:, None] == expert_range[None, :]).astype(jnp.int32)
    host_of = jnp.sum(placed * host_range[:, None], axis=0)
    flat_ids = expert_ids.reshape(-1)
    id_match = flat_ids[:, None] == expert_range[None, :]
    dest_host = jnp.sum(jnp.where(id_match, host_of[None, :], 0), axis=1)
    row_token = jnp.arange(routed, dtype=jnp.int32) // top_count
    padded_tokens = jnp.concatenate([tokens, jnp.zeros((1, width_model), tokens.dtype)], axis=0)
    earlier = (
        lax.broadcasted_iota(jnp.int32, (routed, routed), 0)
        > lax.broadcasted_iota(jnp.int32, (routed, routed), 1)
    ).astype(jnp.bfloat16)
    dest_match = dest_host[:, None] == host_range[None, :]
    before = jnp.dot(earlier, dest_match.astype(jnp.bfloat16), preferred_element_type=jnp.float32)
    position = jnp.sum(jnp.where(dest_match, before, 0.0), axis=1).astype(jnp.int32)
    slot_of_row = dest_host * capacity + position
    source_row = jnp.full((slots + 1,), tok_rows, jnp.int32).at[slot_of_row].set(row_token)[:slots]
    outgoing = padded_tokens[source_row].reshape(hosts, capacity, width_model)
    received = lax.all_to_all(outgoing, "expert", split_axis=0, concat_axis=0, tiled=True)
    flat_in = received.reshape(-1, width_model)
    served = expert_block(flat_in, gate_up, down_proj, hidden_width).reshape(received.shape)
    returned = lax.all_to_all(served, "expert", split_axis=0, concat_axis=0, tiled=True)
    expert_rows = returned.reshape(slots, width_model)[slot_of_row]
    weights = gate_scores / jnp.sum(gate_scores, axis=1, keepdims=True)
    mixed = jnp.sum(
        weights[:, :, None]
        * expert_rows.reshape(tok_rows, top_count, width_model).astype(jnp.float32),
        axis=1,
    )
    return mixed.astype(jnp.bfloat16)


AXES = ("ez", "ex", "ec")


def gather_stage(block, axis, size):
    got = [block]
    for shift in range(1, size):
        pairs = [(i, i ^ shift if size & (size - 1) == 0 else (i + shift) % size) for i in range(size)]
        got.append(lax.ppermute(block, axis, pairs))
    return jnp.concatenate(got, axis=0)


def scatter_stage(part, axis, size):
    pieces = jnp.split(part, size, axis=0)
    total = pieces[0].astype(jnp.float32)
    for shift in range(1, size):
        pairs = [(i, i ^ shift if size & (size - 1) == 0 else (i - shift) % size) for i in range(size)]
        total = total + lax.ppermute(pieces[shift].astype(jnp.bfloat16), axis, pairs).astype(jnp.float32)
    return total


def dense_shards(tokens, expert_ids, gate_scores, host_expert, w_in, w_down):
    tok_rows, width_model = tokens.shape
    hidden_width = w_down.shape[1]
    experts = host_expert.shape[0]
    sizes = [lax.axis_size(a) for a in AXES]
    hosts = sizes[0] * sizes[1] * sizes[2]
    me = (lax.axis_index("ez") * sizes[1] + lax.axis_index("ex")) * sizes[2] + lax.axis_index("ec")
    weights = gate_scores / jnp.sum(gate_scores, axis=1, keepdims=True)
    chosen = expert_ids[:, :, None] == host_expert[None, None, :]
    per_host = jnp.sum(jnp.where(chosen, weights[:, :, None], 0.0), axis=1)
    hi = lax.reduce_precision(per_host, exponent_bits=8, mantissa_bits=7)
    rest = per_host - hi
    lo = lax.reduce_precision(rest, exponent_bits=8, mantissa_bits=7)
    lo2 = rest - lo
    extra = -(-3 * hosts // 128) * 128
    meta = jnp.concatenate([hi, lo, lo2, jnp.zeros((tok_rows, extra - 3 * hosts), jnp.float32)], axis=1)
    meta = meta.astype(jnp.bfloat16)
    carried = jnp.concatenate([tokens, meta], axis=1)
    pick = (jnp.arange(hosts, dtype=jnp.int32) == me).astype(jnp.float32)
    results = []
    held = None
    for rows in jnp.split(carried, STREAMS, axis=0):
        if held is not None:
            held, rows = lax.optimization_barrier((held, rows))
        rows = gather_stage(rows, AXES[0], sizes[0])
        held = rows
        for axis, size in zip(AXES[1:], sizes[1:]):
            rows = gather_stage(rows, axis, size)
        tail = rows[:, width_model:width_model + 3 * hosts].astype(jnp.float32)
        gate = tail[:, :hosts] + tail[:, hosts:2 * hosts] + tail[:, 2 * hosts:]
        mine = jnp.sum(gate * pick[None, :], axis=1)
        out = expert_block(rows[:, :width_model], w_in[0], w_down[0], hidden_width)
        part = out.astype(jnp.float32) * mine[:, None]
        for axis, size in list(zip(AXES, sizes))[::-1]:
            part = scatter_stage(part, axis, size)
        results.append(part)
    return jnp.concatenate(results, axis=0).astype(jnp.bfloat16)


STREAMS = 2


def factor_expert(mesh):
    row = mesh.devices[0]
    try:
        cores = len({d.core_on_chip for d in row})
        xs = len({d.coords[0] for d in row})
        zs = len({d.coords[2] for d in row})
    except AttributeError:
        return None
    if cores * xs * zs != row.shape[0]:
        return None
    return zs, xs, cores


def solution(mesh):
    placed = (
        P(("groups", "expert"), None),
        P(("groups", "expert"), None),
        P(("groups", "expert"), None),
        P(),
        P("expert", None, None),
        P("expert", None, None),
    )
    factors = factor_expert(mesh)
    if factors is None or mesh.shape["expert"] > 16:
        return jax.shard_map(
            shards, mesh=mesh, in_specs=placed, out_specs=P(("groups", "expert"), None), check_vma=False
        )
    sub = Mesh(mesh.devices.reshape((mesh.shape["groups"],) + factors), ("groups",) + AXES)
    rows = P(("groups",) + AXES, None)
    placed = (rows, rows, rows, P(), P(AXES, None, None), P(AXES, None, None))
    return jax.shard_map(dense_shards, mesh=sub, in_specs=placed, out_specs=rows, check_vma=False)
```

```python
import jax
import jax.numpy as jnp
import numpy as np
from jax import lax
from jax.sharding import Mesh, PartitionSpec as P


def expert_block(rows_in, gate_up, down_proj, hidden_width):
    pair = jnp.dot(rows_in, gate_up, preferred_element_type=jnp.float32)
    active = (jax.nn.silu(pair[:, :hidden_width]) * pair[:, hidden_width:]).astype(jnp.bfloat16)
    return jnp.dot(active, down_proj, preferred_element_type=jnp.float32).astype(jnp.bfloat16)


def shards(tokens, expert_ids, gate_scores, host_expert, w_in, w_down):
    tok_rows, width_model = tokens.shape
    top_count = expert_ids.shape[1]
    hosts = lax.axis_size("expert")
    experts = host_expert.shape[0]
    capacity = 3 * tok_rows * top_count // (2 * experts)
    hidden_width = w_down.shape[1]
    routed = tok_rows * top_count
    slots = hosts * capacity
    gate_up = w_in[0]
    down_proj = w_down[0]
    expert_range = jnp.arange(experts, dtype=jnp.int32)
    host_range = jnp.arange(hosts, dtype=jnp.int32)
    placed = (host_expert[:, None] == expert_range[None, :]).astype(jnp.int32)
    host_of = jnp.sum(placed * host_range[:, None], axis=0)
    flat_ids = expert_ids.reshape(-1)
    id_match = flat_ids[:, None] == expert_range[None, :]
    dest_host = jnp.sum(jnp.where(id_match, host_of[None, :], 0), axis=1)
    row_token = jnp.arange(routed, dtype=jnp.int32) // top_count
    padded_tokens = jnp.concatenate([tokens, jnp.zeros((1, width_model), tokens.dtype)], axis=0)
    earlier = (
        lax.broadcasted_iota(jnp.int32, (routed, routed), 0)
        > lax.broadcasted_iota(jnp.int32, (routed, routed), 1)
    ).astype(jnp.bfloat16)
    dest_match = dest_host[:, None] == host_range[None, :]
    before = jnp.dot(earlier, dest_match.astype(jnp.bfloat16), preferred_element_type=jnp.float32)
    position = jnp.sum(jnp.where(dest_match, before, 0.0), axis=1).astype(jnp.int32)
    slot_of_row = dest_host * capacity + position
    source_row = jnp.full((slots + 1,), tok_rows, jnp.int32).at[slot_of_row].set(row_token)[:slots]
    outgoing = padded_tokens[source_row].reshape(hosts, capacity, width_model)
    received = lax.all_to_all(outgoing, "expert", split_axis=0, concat_axis=0, tiled=True)
    flat_in = received.reshape(-1, width_model)
    served = expert_block(flat_in, gate_up, down_proj, hidden_width).reshape(received.shape)
    returned = lax.all_to_all(served, "expert", split_axis=0, concat_axis=0, tiled=True)
    expert_rows = returned.reshape(slots, width_model)[slot_of_row]
    weights = gate_scores / jnp.sum(gate_scores, axis=1, keepdims=True)
    mixed = jnp.sum(
        weights[:, :, None]
        * expert_rows.reshape(tok_rows, top_count, width_model).astype(jnp.float32),
        axis=1,
    )
    return mixed.astype(jnp.bfloat16)


AXES = ("ez", "ex", "ec")


def gather_stage(block, axis, size):
    got = [block]
    for shift in range(1, size):
        pairs = [(i, (i + shift) % size) for i in range(size)]
        got.append(lax.ppermute(block, axis, pairs))
    return jnp.concatenate(got, axis=0)


def scatter_stage(part, axis, size):
    pieces = jnp.split(part, size, axis=0)
    total = pieces[0].astype(jnp.float32)
    for shift in range(1, size):
        pairs = [(i, (i - shift) % size) for i in range(size)]
        total = total + lax.ppermute(pieces[shift].astype(jnp.bfloat16), axis, pairs).astype(jnp.float32)
    return total


def dense_shards(tokens, expert_ids, gate_scores, host_expert, w_in, w_down):
    tok_rows, width_model = tokens.shape
    hidden_width = w_down.shape[1]
    experts = host_expert.shape[0]
    sizes = [lax.axis_size(a) for a in AXES]
    hosts = sizes[0] * sizes[1] * sizes[2]
    me = (lax.axis_index("ez") * sizes[1] + lax.axis_index("ex")) * sizes[2] + lax.axis_index("ec")
    weights = gate_scores / jnp.sum(gate_scores, axis=1, keepdims=True)
    chosen = expert_ids[:, :, None] == host_expert[None, None, :]
    per_host = jnp.sum(jnp.where(chosen, weights[:, :, None], 0.0), axis=1)
    hi = lax.reduce_precision(per_host, exponent_bits=8, mantissa_bits=7)
    rest = per_host - hi
    lo = lax.reduce_precision(rest, exponent_bits=8, mantissa_bits=7)
    lo2 = rest - lo
    extra = -(-3 * hosts // 128) * 128
    meta = jnp.concatenate([hi, lo, lo2, jnp.zeros((tok_rows, extra - 3 * hosts), jnp.float32)], axis=1)
    meta = meta.astype(jnp.bfloat16)
    carried = jnp.concatenate([tokens, meta], axis=1)
    pick = (jnp.arange(hosts, dtype=jnp.int32) == me).astype(jnp.float32)
    results = []
    held = None
    crossed = None
    for rows in jnp.split(carried, STREAMS, axis=0):
        if held is not None:
            held, rows = lax.optimization_barrier((held, rows))
        rows = gather_stage(rows, AXES[0], sizes[0])
        if crossed is not None:
            crossed, rows = lax.optimization_barrier((crossed, rows))
        held = rows
        rows = gather_stage(rows, AXES[1], sizes[1])
        crossed = rows
        rows = gather_stage(rows, AXES[2], sizes[2])
        tail = rows[:, width_model:width_model + 3 * hosts].astype(jnp.float32)
        gate = tail[:, :hosts] + tail[:, hosts:2 * hosts] + tail[:, 2 * hosts:]
        mine = jnp.sum(gate * pick[None, :], axis=1)
        out = expert_block(rows[:, :width_model], w_in[0], w_down[0], hidden_width)
        part = out.astype(jnp.float32) * mine[:, None]
        for axis, size in list(zip(AXES, sizes))[::-1]:
            part = scatter_stage(part, axis, size)
        results.append(part)
    return jnp.concatenate(results, axis=0).astype(jnp.bfloat16)


STREAMS = 2


def factor_expert(mesh):
    row = mesh.devices[0]
    try:
        cores = len({d.core_on_chip for d in row})
        xs = len({d.coords[0] for d in row})
        zs = len({d.coords[2] for d in row})
    except AttributeError:
        return None
    if cores * xs * zs != row.shape[0]:
        return None
    return zs, xs, cores


def solution(mesh):
    placed = (
        P(("groups", "expert"), None),
        P(("groups", "expert"), None),
        P(("groups", "expert"), None),
        P(),
        P("expert", None, None),
        P("expert", None, None),
    )
    factors = factor_expert(mesh)
    if factors is None or mesh.shape["expert"] > 16:
        return jax.shard_map(
            shards, mesh=mesh, in_specs=placed, out_specs=P(("groups", "expert"), None), check_vma=False
        )
    sub = Mesh(mesh.devices.reshape((mesh.shape["groups"],) + factors), ("groups",) + AXES)
    rows = P(("groups",) + AXES, None)
    placed = (rows, rows, rows, P(), P(AXES, None, None), P(AXES, None, None))
    return jax.shard_map(dense_shards, mesh=sub, in_specs=placed, out_specs=rows, check_vma=False)
```
